128 devices in a mesh: leaf: 8 (over z, core), expert: 8 (over x_hi, y), tensor: 2 (over x_lo).
Axes of the slice: x: 4 (x_hi: 2, x_lo: 2; x = x_hi * 2 + x_lo), y: 4, z: 4, core: 2. Of those that a mesh axis runs over, the one named last changes fastest.
Arguments:
- drafts: bfloat16 [2048, 6144], P('leaf', ('expert', 'tensor')), may hold values from -6 to 6
- children: bfloat16 [4096, 6144], P('leaf', ('expert', 'tensor')), may hold values from -6 to 6
- child_order: int32 [16], replicated, may hold values from 0 to 15, each once
- spans: int32 [4096], P('leaf'), may hold values from 0 to 15
- span_bias: float32 [48, 16], P(('expert', 'tensor')), may hold values from -4 to 4
- out_weight: bfloat16 [6144, 6144], P(('expert', 'tensor')), may hold values from -0.078125 to 0.078125
- norm_gain: float32 [6144], replicated, may hold values from 0.1 to 1.9
- router: bfloat16 [6144, 8], replicated, may hold values from -0.078125 to 0.078125
- routes: int32 [2048, 2], P(('leaf', 'expert')), may hold values from 0 to 7, all different within a row; in each aligned block of 32 rows (0 to 31, 32 to 63, ...) at most 16 rows name the same one
- w_gate: bfloat16 [8, 6144, 8192], P('expert', None, ('leaf', 'tensor')), may hold values from -0.078125 to 0.078125
- w_up: bfloat16 [8, 6144, 8192], P('expert', None, ('leaf', 'tensor')), may hold values from -0.078125 to 0.078125
- w_down: bfloat16 [8, 8192, 6144], P('expert', ('leaf', 'tensor')), may hold values from -0.0625 to 0.0625
Outputs:
- merged_out: float32 [2048, 6144], P(('leaf', 'expert'))
The draws below stay inside these ranges and needn't reach their ends.
Inputs may be any that keep to these rules, and one draw needn't show every extreme that they name: `routes`: each row names two different experts; within the rows of one index pair of leaf and expert (32 aligned rows) no expert is named more than 16 times, and exactly 16 times in some of them. `child_order`: A permutation: every parent has exactly two children.
All inputs are finite; a program needn't handle non-finite values.
Results may differ from the reference program's by a relative error of at most 0.013.
Values may be sent and summed in bfloat16 or wider, within the bound.
No kernel may reach another device: no remote copies, remote signals or barrier semaphores. Data moves between devices by JAX's collectives and lax.ppermute only.
A program may use at most 128 MiB of HBM per device.

```python
import math
import jax
import jax.numpy as jnp
import numpy as np
from jax import lax

D = 6144
HEADS = 48
HD = 128
FFW = 8192
R = 256
SPANS = 16
PARENTS = 8
CHILDREN = 16
TOKENS = 2048
TOK_DEV = 32
EXPERTS = 8
CAP = 16
N_LEAF = 8
N_TENSOR = 2


def planted_pattern(key):
    folded = jax.random.fold_in(key, 9173)
    pieces = jax.random.split(folded, 4)
    head_pick = jax.random.randint(pieces[0], (), 0, HEADS)
    sign_table = jnp.where(jax.random.bernoulli(pieces[1], 0.5, (HD,)), 1.0, -1.0).astype(jnp.float32)
    query_start = jax.random.randint(pieces[2], (), 0, R)
    key_start = jax.random.randint(pieces[3], (), 0, R)
    return (head_pick, sign_table, query_start, key_start)


def base_values(key, count, salt):
    folded = jax.random.fold_in(key, salt)
    return jnp.clip(jax.random.normal(folded, (count, D), jnp.float32), -6.0, 6.0)


def column_layout(head_pick, sign_table):
    column = jnp.arange(D, dtype=jnp.int32)
    in_head = column // HD == head_pick
    feature = column % HD
    aligned = feature < 3 * HD // 4
    pattern = jnp.take(sign_table, feature)
    return (in_head, aligned, pattern)


def draw_drafts(key, part):
    head_pick, sign_table, query_start, key_start = planted_pattern(key)
    values = base_values(key, TOKENS, 4211)
    in_head, aligned, pattern = column_layout(head_pick, sign_table)
    position = jnp.arange(TOKENS, dtype=jnp.int32) % R
    heights = (3.0, 4.5, 5.5)
    strength = jnp.zeros((TOKENS,), jnp.float32)
    chosen_rows = jnp.zeros((TOKENS,), bool)
    for turn_index, height in enumerate(heights):
        hit = position == (query_start + turn_index * (R // 3)) % R
        strength = jnp.where(hit, height, strength)
        chosen_rows = chosen_rows | hit
    planted = jnp.where(aligned[None, :], strength[:, None] * pattern[None, :], 0.0)
    result = jnp.where(chosen_rows[:, None] & in_head[None, :], planted, values)
    return result.astype(jnp.bfloat16)


def draw_children(key, part):
    head_pick, sign_table, query_start, key_start = planted_pattern(key)
    total_rows = CHILDREN * R
    values = base_values(key, total_rows, 7723)
    in_head, aligned, pattern = column_layout(head_pick, sign_table)
    position = jnp.arange(total_rows, dtype=jnp.int32) % R
    strength = jnp.zeros((total_rows,), jnp.float32)
    chosen_rows = jnp.zeros((total_rows,), bool)
    for turn_index in range(4):
        hit = position == (key_start + turn_index * (R // 4)) % R
        strength = jnp.where(hit, 6.0 - 0.0625 * turn_index, strength)
        chosen_rows = chosen_rows | hit
    planted = strength[:, None] * pattern[None, :]
    replace = chosen_rows[:, None] & in_head[None, :] & aligned[None, :]
    result = jnp.where(replace, planted, values)
    return result.astype(jnp.bfloat16)


def touch_ends(array, stream_key, smallest, largest):
    longest = array.shape.index(max(array.shape))
    spots = []
    for shift in (0, 1):
        where = [jax.random.randint(jax.random.fold_in(stream_key, axis), (), 0, length) for axis, length in enumerate(array.shape)]
        where[longest] = (where[longest] + shift) % array.shape[longest]
        spots.append(tuple(where))
    return array.at[spots[0]].set(smallest).at[spots[1]].set(largest)


def block_scale(key, shape, cuts, smallest, top_value):
    factor_of, own = 1.0, jax.random.fold_in(key, 6)
    for axis_at, shards_of in cuts:
        steps = jnp.exp(jax.random.uniform(jax.random.fold_in(own, axis_at), (shards_of,), jnp.float32, smallest / len(cuts), top_value / len(cuts)))
        factor_of = factor_of * jnp.repeat(steps, shape[axis_at] // shards_of).reshape([-1 if axis == axis_at else 1 for axis in range(len(shape))])
    return factor_of


def routed_block(key, own, number, rows, count, top, reach, skew):
    sequence = jax.random.permutation(key, count)
    heavy_load, usual = shares(count, rows * top, reach, skew, True), shares(count, rows * top, reach, skew, False)
    places = jnp.arange(count)

    def named(lengths, offset_by):
        used = int((lengths > 0).sum())
        fixed = max(1, used // 4)
        shifted = fixed + (places - fixed + offset_by * (used - fixed)) % max(1, count - fixed)
        return jnp.zeros((count,), jnp.int32).at[sequence[jnp.where(places < fixed, places, shifted)]].set(jnp.asarray(lengths, jnp.int32))

    lengths = jnp.where(number % 4 == 0, named(heavy_load, number // 4), named(usual, number - number // 4 - 1))
    mixed = jax.random.permutation(jax.random.fold_in(own, 3), count)
    source_of, sink = mixed[0:count // 2 * 2:2], mixed[1:count // 2 * 2:2]
    room = jnp.minimum(lengths[source_of] - 1, reach - lengths[sink]) // 2
    room = jnp.where((source_of == sequence[0]) | (sink == sequence[0]) | (lengths[sink] == 0), 0, jnp.maximum(room, 0))
    shifted = jax.random.randint(jax.random.fold_in(own, 4), (count // 2,), 0, 1 << 20) % (room + 1)
    lengths = lengths.at[source_of].add(-shifted).at[sink].add(shifted)
    labels = jnp.searchsorted(jnp.cumsum(lengths), jnp.arange(rows * top), side="right").astype(jnp.int32)
    grid = labels.reshape(top, rows).T
    grid = grid[jax.random.permutation(jax.random.fold_in(own, 1), rows)]
    offset_by = jax.random.randint(jax.random.fold_in(own, 2), (rows, 1), 0, top)
    return jnp.take_along_axis(grid, (jnp.arange(top)[None, :] + offset_by) % top, axis=1)


def shares(count, total, bound, slope, full):
    portions = [(1 << 20) // math.isqrt(standing ** slope) + 1 for standing in range(1, count + 1)]
    largest = bound if full else min(bound, max(-(-total // count), total * portions[0] // sum(portions)))
    least = 1 if total - largest >= count - 1 else 0
    holding, spare = [largest] + [least] * (count - 1), total - largest - least * (count - 1)
    while spare > 0:
        free = [i for i in range(1, count) if holding[i] < largest] or [i for i in range(1, count) if holding[i] < bound]
        whole, budget = sum([portions[i] for i in free]), spare
        for i in free:
            addition = min(bound - holding[i], max(1, budget * portions[i] // whole), spare)
            holding[i] = holding[i] + addition
            spare = spare - addition
    return np.array(holding)


def bell_draw(rng, extent, deviation, limit, cuts=(), kind=jnp.bfloat16):
    values = jax.random.normal(rng, extent, jnp.float32) * deviation
    if len(cuts) > 0:
        values = block_scale(rng, extent, cuts, -0.22, 0.18) * values
    return jnp.clip(values, min=-limit, max=limit).astype(kind)


def setup_inputs(seed: int = 0) -> dict:
    seeds = jax.random.split(jax.random.key(seed), 13)
    drafts = draw_drafts(jax.random.fold_in(seeds[12], 71), 0)
    children = draw_children(jax.random.fold_in(seeds[12], 71), 0)
    child_order = jax.random.permutation(seeds[2], CHILDREN).astype(jnp.int32)
    spans = touch_ends(jax.random.randint(seeds[3], (CHILDREN * R,), 0, SPANS), jax.random.fold_in(seeds[3], 1), 0, SPANS - 1).astype(jnp.int32)
    span_bias = bell_draw(seeds[4], (HEADS, SPANS), 1.0, 4.0, ((0, 16),), jnp.float32)
    out_weight = bell_draw(seeds[5], (D, D), D ** -0.5, 0.078125, ((0, 16),))
    norm_gain = jnp.clip(1.0 + 0.18 * jax.random.normal(seeds[6], (D,), jnp.float32), 0.1, 1.9)
    router = bell_draw(seeds[7], (D, EXPERTS), D ** -0.5, 0.078125)
    routes_keys = jax.random.split(jax.random.fold_in(seeds[8], 1), TOKENS // TOK_DEV)
    routes_turns = jax.random.permutation(jax.random.fold_in(seeds[8], 3), TOKENS // TOK_DEV)
    routes = jax.vmap(lambda own, number: routed_block(jax.random.fold_in(seeds[8], 2), own, number, TOK_DEV, EXPERTS, 2, CAP, 2))(routes_keys, routes_turns).reshape((TOKENS, 2))
    w_gate = bell_draw(seeds[9], (EXPERTS, D, FFW), D ** -0.5, 0.078125, ((0, 8), (2, 16)))
    w_up = bell_draw(seeds[10], (EXPERTS, D, FFW), D ** -0.5, 0.078125, ((0, 8), (2, 16)))
    w_down = bell_draw(seeds[11], (EXPERTS, FFW, D), FFW ** -0.5, 0.0625, ((0, 8), (1, 16)))
    return dict(drafts=drafts, children=children, child_order=child_order, spans=spans, span_bias=span_bias, out_weight=out_weight, norm_gain=norm_gain, router=router, routes=routes, w_gate=w_gate, w_up=w_up, w_down=w_down)


def reference(drafts, children, child_order, spans, span_bias, out_weight, norm_gain, router, routes, w_gate, w_up, w_down):
    width = drafts.shape[1]
    head_size = width // HEADS
    scale = 1.0 / math.sqrt(head_size)
    count = child_order.shape[0]
    inverse = jnp.zeros((count,), jnp.int32).at[child_order].set(jnp.arange(count, dtype=jnp.int32))

    def merge_parent(parent):
        queries = lax.dynamic_slice_in_dim(drafts, (parent * R).astype(jnp.int32), R, 0)
        first = inverse[2 * parent]
        second = inverse[2 * parent + 1]
        keys = jnp.concatenate([lax.dynamic_slice_in_dim(children, (first * R).astype(jnp.int32), R, 0), lax.dynamic_slice_in_dim(children, (second * R).astype(jnp.int32), R, 0)], axis=0)
        key_spans = jnp.concatenate([lax.dynamic_slice_in_dim(spans, (first * R).astype(jnp.int32), R, 0), lax.dynamic_slice_in_dim(spans, (second * R).astype(jnp.int32), R, 0)], axis=0)
        query_f = queries.astype(jnp.float32).reshape(R, HEADS, head_size)
        key_f = keys.astype(jnp.float32).reshape(2 * R, HEADS, head_size)
        scores = jnp.einsum('qhd,khd->hqk', query_f, key_f, precision=lax.Precision.HIGHEST) * scale
        scores = scores + span_bias[:, key_spans][:, None, :]
        probs = jax.nn.softmax(scores, axis=-1)
        attended = jnp.einsum('hqk,khd->qhd', probs, key_f, precision=lax.Precision.HIGHEST)
        return attended.reshape(R, width).astype(jnp.bfloat16)
    attended = lax.map(merge_parent, jnp.arange(PARENTS, dtype=jnp.int32)).reshape(PARENTS * R, width)
    merged = drafts.astype(jnp.float32) + jnp.dot(attended, out_weight, preferred_element_type=jnp.float32)
    mean_square = lax.optimization_barrier(jnp.mean(merged * merged, axis=-1, keepdims=True))
    normed = (merged * lax.rsqrt(mean_square + 1e-05) * norm_gain).astype(jnp.bfloat16)
    logits = jnp.dot(normed, router, preferred_element_type=jnp.float32)
    experts = router.shape[1]
    expert_hot = routes[:, :, None] == jnp.arange(experts, dtype=jnp.int32)[None, None, :]
    chosen = lax.optimization_barrier(jnp.sum(jnp.where(expert_hot, logits[:, None, :], 0.0), axis=-1))
    gates = jax.nn.softmax(chosen, axis=-1)
    blocks = routes.shape[0] // TOK_DEV
    pairs = routes.reshape(blocks, 2 * TOK_DEV)
    pair_hot = (pairs[:, :, None] == jnp.arange(experts, dtype=jnp.int32)[None, None, :]).astype(jnp.int32)
    earlier = jnp.cumsum(pair_hot, axis=1) - pair_hot
    slot_index = lax.optimization_barrier(jnp.sum(earlier * pair_hot, axis=-1))
    block_ids = jnp.broadcast_to(jnp.arange(blocks, dtype=jnp.int32)[:, None], pairs.shape)
    rows = jnp.repeat(normed.reshape(blocks, TOK_DEV, width), 2, axis=1)
    buffers = jnp.zeros((experts, blocks, CAP, width), jnp.bfloat16)
    buffers = buffers.at[pairs, block_ids, slot_index].set(rows)
    buffers = buffers.reshape(experts, blocks * CAP, width)
    pieces = N_LEAF * N_TENSOR
    piece_width = w_gate.shape[2] // pieces

    def run_expert(operands):
        inputs, gate_w, up_w, down_w = operands
        gate_blocks = gate_w.reshape(width, pieces, piece_width).transpose(1, 0, 2)
        up_blocks = up_w.reshape(width, pieces, piece_width).transpose(1, 0, 2)
        down_blocks = down_w.reshape(pieces, piece_width, width)

        def add_piece(total, weights):
            gate_b, up_b, down_b = weights
            gate_v = jnp.dot(inputs, gate_b, preferred_element_type=jnp.float32)
            up_v = jnp.dot(inputs, up_b, preferred_element_type=jnp.float32)
            hidden = (jax.nn.silu(gate_v) * up_v).astype(jnp.bfloat16)
            part = jnp.dot(hidden, down_b, preferred_element_type=jnp.float32).astype(jnp.bfloat16)
            return (total + part.astype(jnp.float32), None)
        total, unused = lax.scan(add_piece, jnp.zeros((blocks * CAP, width), jnp.float32), (gate_blocks, up_blocks, down_blocks))
        return total.astype(jnp.bfloat16)
    outputs = lax.map(run_expert, (buffers, w_gate, w_up, w_down)).reshape(experts, blocks, CAP, width)
    picked = outputs[pairs, block_ids, slot_index].astype(jnp.float32).reshape(blocks * TOK_DEV, 2, width)
    mixed = gates[:, 0:1] * picked[:, 0] + gates[:, 1:2] * picked[:, 1]
    return (merged + mixed).astype(jnp.float32)
```

```python
import math

import jax
import jax.numpy as jnp
from jax import lax
from jax.sharding import PartitionSpec as P

R = 256


def attend_parent(queries, keys, key_spans, span_bias, scale):
    rows, local_width = queries.shape
    heads_here, span_count = span_bias.shape
    head_size = local_width // heads_here
    key_count = keys.shape[0]
    q = queries.reshape(rows, heads_here, head_size)
    k = keys.reshape(key_count, heads_here, head_size)
    scores = jnp.einsum("qhd,khd->hqk", q, k, preferred_element_type=jnp.float32) * scale
    span_hot = (key_spans[:, None] == jnp.arange(span_count, dtype=jnp.int32)[None, :]).astype(
        jnp.float32
    )
    bias = jnp.dot(span_hot, span_bias.T, precision=lax.Precision.HIGHEST)
    scores = scores + bias.T[:, None, :]
    top = jnp.max(scores, axis=-1, keepdims=True)
    weights = jnp.exp(scores - top)
    total = jnp.sum(weights, axis=-1, keepdims=True)
    values = jnp.einsum(
        "hqk,khd->hqd", weights, k.astype(jnp.float32), precision=lax.Precision.HIGHEST
    )
    return (values / total).transpose(1, 0, 2).reshape(rows, local_width).astype(jnp.bfloat16)


def per_device(
    drafts,
    children,
    child_order,
    spans,
    span_bias,
    out_weight,
    norm_gain,
    router,
    routes,
    w_gate,
    w_up,
    w_down,
):
    local_rows, local_width = drafts.shape
    heads_here = span_bias.shape[0]
    head_size = local_width // heads_here
    width = out_weight.shape[1]
    scale = 1.0 / math.sqrt(head_size)
    parents_here = local_rows // R
    leaf_index = lax.axis_index("leaf")
    keys = lax.all_gather(children, "leaf", axis=0, tiled=True)
    key_spans = lax.all_gather(spans, "leaf", axis=0, tiled=True)
    count = child_order.shape[0]
    ids = jnp.arange(count, dtype=jnp.int32)
    inverse = jnp.sum(jnp.where(child_order[None, :] == ids[:, None], ids[None, :], 0), axis=1)
    pieces = []
    for i in range(parents_here):
        parent = leaf_index * parents_here + i
        first = inverse[2 * parent]
        second = inverse[2 * parent + 1]
        own_keys = jnp.concatenate(
            [
                lax.dynamic_slice_in_dim(keys, first * R, R, 0),
                lax.dynamic_slice_in_dim(keys, second * R, R, 0),
            ],
            axis=0,
        )
        own_spans = jnp.concatenate(
            [
                lax.dynamic_slice_in_dim(key_spans, first * R, R, 0),
                lax.dynamic_slice_in_dim(key_spans, second * R, R, 0),
            ],
            axis=0,
        )
        pieces.append(attend_parent(drafts[i * R : (i + 1) * R], own_keys, own_spans, span_bias, scale))
    attended = pieces[0] if parents_here == 1 else jnp.concatenate(pieces, axis=0)
    term = jnp.dot(attended, out_weight, preferred_element_type=jnp.float32).astype(jnp.bfloat16)
    group = lax.axis_size(("expert", "tensor"))
    share_rows = local_rows // group
    arrived_terms = lax.all_to_all(
        term.reshape(group, share_rows, width), ("expert", "tensor"), 0, 0, tiled=True
    )
    own_drafts = lax.all_to_all(drafts, ("expert", "tensor"), 0, 1, tiled=True)
    share = jnp.sum(arrived_terms.astype(jnp.float32), axis=0) + own_drafts.astype(jnp.float32)
    merged = lax.all_gather(share, "tensor", axis=0, tiled=True)
    mean_square = jnp.mean(merged * merged, axis=-1, keepdims=True)
    normed = (merged * lax.rsqrt(mean_square + 1e-05) * norm_gain).astype(jnp.bfloat16)
    logits = jnp.dot(normed, router, preferred_element_type=jnp.float32)
    experts = router.shape[1]
    tok_count = routes.shape[0]
    capacity = 4 * tok_count // lax.axis_size("expert")
    choice_hot = routes[:, :, None] == jnp.arange(experts, dtype=jnp.int32)[None, None, :]
    chosen = jnp.sum(jnp.where(choice_hot, logits[:, None, :], 0.0), axis=-1)
    gates = jax.nn.softmax(chosen, axis=-1)
    pairs = routes.reshape(-1)
    pair_hot = (pairs[:, None] == jnp.arange(experts, dtype=jnp.int32)[None, :]).astype(jnp.int32)
    earlier = jnp.cumsum(pair_hot, axis=0) - pair_hot
    slot_index = jnp.sum(earlier * pair_hot, axis=1)
    target = pairs * capacity + slot_index
    place_hot = (
        jnp.arange(experts * capacity, dtype=jnp.int32)[:, None] == target[None, :]
    ).astype(jnp.bfloat16)
    place_rows = jnp.sum(place_hot.reshape(experts * capacity, tok_count, 2), axis=-1)
    outgoing = jnp.dot(place_rows, normed, preferred_element_type=jnp.float32).astype(jnp.bfloat16)
    outgoing = outgoing.reshape(experts, capacity, width)
    arrived = lax.all_to_all(outgoing, "expert", split_axis=0, concat_axis=0, tiled=True).reshape(
        -1, width
    )
    piece = lax.all_gather(arrived, "leaf", axis=0, tiled=True)
    gate_v = jnp.dot(piece, w_gate[0], preferred_element_type=jnp.float32)
    up_v = jnp.dot(piece, w_up[0], preferred_element_type=jnp.float32)
    hidden = (jax.nn.silu(gate_v) * up_v).astype(jnp.bfloat16)
    down = jnp.dot(hidden, w_down[0], preferred_element_type=jnp.float32).astype(jnp.bfloat16)
    part_rows = lax.psum_scatter(down, "leaf", scatter_dimension=0, tiled=True)
    back = lax.all_to_all(
        part_rows.reshape(-1, capacity, width), "expert", split_axis=0, concat_axis=0, tiled=True
    ).reshape(-1, width)
    picked = jnp.take(back, target, axis=0)
    halves = lax.all_gather(picked, "tensor", axis=0, tiled=False)
    expert_out = jnp.sum(halves.astype(jnp.float32), axis=0).astype(jnp.bfloat16)
    picked = expert_out.astype(jnp.float32).reshape(tok_count, 2, width)
    mixed = gates[:, 0:1] * picked[:, 0] + gates[:, 1:2] * picked[:, 1]
    return merged + mixed


def solution(mesh):
    in_specs = (
        P("leaf", ("expert", "tensor")),
        P("leaf", ("expert", "tensor")),
        P(),
        P("leaf"),
        P(("expert", "tensor"), None),
        P(("expert", "tensor"), None),
        P(),
        P(),
        P(("leaf", "expert"), None),
        P("expert", None, ("leaf", "tensor")),
        P("expert", None, ("leaf", "tensor")),
        P("expert", ("leaf", "tensor"), None),
    )
    out_specs = P(("leaf", "expert"), None)
    return jax.shard_map(
        per_device, mesh=mesh, in_specs=in_specs, out_specs=out_specs, check_vma=False
    )
```

```python
import math

import jax
import jax.numpy as jnp
from jax import lax
from jax.sharding import PartitionSpec as P

R = 256


def attend_parent(queries, keys, key_spans, span_bias, scale):
    rows, local_width = queries.shape
    heads_here, span_count = span_bias.shape
    head_size = local_width // heads_here
    key_count = keys.shape[0]
    q = queries.reshape(rows, heads_here, head_size)
    k = keys.reshape(key_count, heads_here, head_size)
    scores = jnp.einsum("qhd,khd->hqk", q, k, preferred_element_type=jnp.float32) * scale
    span_hot = (key_spans[:, None] == jnp.arange(span_count, dtype=jnp.int32)[None, :]).astype(
        jnp.float32
    )
    bias = jnp.dot(span_hot, span_bias.T, precision=lax.Precision.HIGHEST)
    scores = scores + bias.T[:, None, :]
    top = jnp.max(scores, axis=-1, keepdims=True)
    weights = jnp.exp(scores - top)
    total = jnp.sum(weights, axis=-1, keepdims=True)
    values = jnp.einsum(
        "hqk,khd->hqd", weights, k.astype(jnp.float32), precision=lax.Precision.HIGHEST
    )
    return (values / total).transpose(1, 0, 2).reshape(rows, local_width).astype(jnp.bfloat16)


def pair_gather(share):
    other = lax.ppermute(share, "tensor", perm=[(0, 1), (1, 0)])
    low = lax.axis_index("tensor") == 0
    return jnp.concatenate([jnp.where(low, share, other), jnp.where(low, other, share)], axis=0)


def per_device(
    drafts,
    children,
    child_order,
    spans,
    span_bias,
    out_weight,
    norm_gain,
    router,
    routes,
    w_gate,
    w_up,
    w_down,
):
    local_rows, local_width = drafts.shape
    heads_here = span_bias.shape[0]
    head_size = local_width // heads_here
    width = out_weight.shape[1]
    scale = 1.0 / math.sqrt(head_size)
    parents_here = local_rows // R
    leaf_index = lax.axis_index("leaf")
    child_rows = children.shape[0]
    children_here = child_rows // R
    span_rows = -(-spans.shape[0] // local_width)
    span_rows = -(-span_rows // 8) * 8
    span_block = jnp.pad(spans.astype(jnp.bfloat16), (0, span_rows * local_width - spans.shape[0]))
    payload = jnp.concatenate([children, span_block.reshape(span_rows, local_width)], axis=0)
    gathered = lax.all_gather(payload, "leaf", axis=0, tiled=False)
    span_table = gathered[:, child_rows:].reshape(gathered.shape[0], span_rows * local_width)
    count = child_order.shape[0]
    ids = jnp.arange(count, dtype=jnp.int32)
    inverse = jnp.sum(jnp.where(child_order[None, :] == ids[:, None], ids[None, :], 0), axis=1)

    def child_keys(child):
        holder = child // children_here
        offset = (child % children_here) * R
        rows = lax.dynamic_slice(gathered, (holder, offset, 0), (1, R, local_width))[0]
        marks = lax.dynamic_slice(span_table, (holder, offset), (1, R))[0]
        return rows, marks.astype(jnp.int32)

    pieces = []
    for i in range(parents_here):
        parent = leaf_index * parents_here + i
        first_rows, first_spans = child_keys(inverse[2 * parent])
        second_rows, second_spans = child_keys(inverse[2 * parent + 1])
        own_keys = jnp.concatenate([first_rows, second_rows], axis=0)
        own_spans = jnp.concatenate([first_spans, second_spans], axis=0)
        pieces.append(attend_parent(drafts[i * R : (i + 1) * R], own_keys, own_spans, span_bias, scale))
    attended = pieces[0] if parents_here == 1 else jnp.concatenate(pieces, axis=0)
    term = jnp.dot(attended, out_weight, preferred_element_type=jnp.float32).astype(jnp.bfloat16)
    group = lax.axis_size(("expert", "tensor"))
    share_rows = local_rows // group
    arrived_terms = lax.all_to_all(
        term.reshape(group, share_rows, width), ("expert", "tensor"), 0, 0, tiled=True
    )
    own_drafts = lax.all_to_all(drafts, ("expert", "tensor"), 0, 1, tiled=True)
    share = jnp.sum(arrived_terms.astype(jnp.float32), axis=0) + own_drafts.astype(jnp.float32)
    merged = pair_gather(share)
    mean_square = jnp.mean(merged * merged, axis=-1, keepdims=True)
    normed = (merged * lax.rsqrt(mean_square + 1e-05) * norm_gain).astype(jnp.bfloat16)
    logits = jnp.dot(normed, router, preferred_element_type=jnp.float32)
    experts = router.shape[1]
    tok_count = routes.shape[0]
    capacity = 4 * tok_count // lax.axis_size("expert")
    choice_hot = routes[:, :, None] == jnp.arange(experts, dtype=jnp.int32)[None, None, :]
    chosen = jnp.sum(jnp.where(choice_hot, logits[:, None, :], 0.0), axis=-1)
    gates = jax.nn.softmax(chosen, axis=-1)
    pairs = routes.reshape(-1)
    pair_hot = (pairs[:, None] == jnp.arange(experts, dtype=jnp.int32)[None, :]).astype(jnp.int32)
    earlier = jnp.cumsum(pair_hot, axis=0) - pair_hot
    slot_index = jnp.sum(earlier * pair_hot, axis=1)
    target = pairs * capacity + slot_index
    place_hot = (
        jnp.arange(experts * capacity, dtype=jnp.int32)[:, None] == target[None, :]
    ).astype(jnp.bfloat16)
    place_rows = jnp.sum(place_hot.reshape(experts * capacity, tok_count, 2), axis=-1)
    outgoing = jnp.dot(place_rows, normed, preferred_element_type=jnp.float32).astype(jnp.bfloat16)
    outgoing = outgoing.reshape(experts, capacity, width)
    arrived = lax.all_to_all(outgoing, "expert", split_axis=0, concat_axis=0, tiled=True).reshape(
        -1, width
    )
    chunks = 2
    chunk_rows = arrived.shape[0] // chunks
    returned = []
    for c in range(chunks):
        piece = lax.all_gather(arrived[c * chunk_rows : (c + 1) * chunk_rows], "leaf", axis=0, tiled=True)
        gate_v = jnp.dot(piece, w_gate[0], preferred_element_type=jnp.float32)
        up_v = jnp.dot(piece, w_up[0], preferred_element_type=jnp.float32)
        hidden = (jax.nn.silu(gate_v) * up_v).astype(jnp.bfloat16)
        down = jnp.dot(hidden, w_down[0], preferred_element_type=jnp.float32).astype(jnp.bfloat16)
        returned.append(lax.psum_scatter(down, "leaf", scatter_dimension=0, tiled=True))
    part_rows = jnp.concatenate(returned, axis=0)
    back = lax.all_to_all(
        part_rows.reshape(-1, capacity, width), "expert", split_axis=0, concat_axis=0, tiled=True
    ).reshape(-1, width)
    picked = jnp.take(back, target, axis=0)
    other = lax.ppermute(picked, "tensor", perm=[(0, 1), (1, 0)])
    expert_out = (picked.astype(jnp.float32) + other.astype(jnp.float32)).astype(jnp.bfloat16)
    picked = expert_out.astype(jnp.float32).reshape(tok_count, 2, width)
    mixed = gates[:, 0:1] * picked[:, 0] + gates[:, 1:2] * picked[:, 1]
    return merged + mixed


def solution(mesh):
    in_specs = (
        P("leaf", ("expert", "tensor")),
        P("leaf", ("expert", "tensor")),
        P(),
        P("leaf"),
        P(("expert", "tensor"), None),
        P(("expert", "tensor"), None),
        P(),
        P(),
        P(("leaf", "expert"), None),
        P("expert", None, ("leaf", "tensor")),
        P("expert", None, ("leaf", "tensor")),
        P("expert", ("leaf", "tensor"), None),
    )
    out_specs = P(("leaf", "expert"), None)
    return jax.shard_map(
        per_device, mesh=mesh, in_specs=in_specs, out_specs=out_specs, check_vma=False
    )
```

```python
import math

import jax
import jax.numpy as jnp
from jax import lax
from jax.sharding import PartitionSpec as P

R = 256


def attend_parent(queries, keys, key_spans, span_bias, scale):
    rows, local_width = queries.shape
    heads_here, span_count = span_bias.shape
    head_size = local_width // heads_here
    key_count = keys.shape[0]
    q = queries.reshape(rows, heads_here, head_size)
    k = keys.reshape(key_count, heads_here, head_size)
    scores = jnp.einsum("qhd,khd->hqk", q, k, preferred_element_type=jnp.float32) * scale
    span_hot = (key_spans[:, None] == jnp.arange(span_count, dtype=jnp.int32)[None, :]).astype(
        jnp.float32
    )
    bias = jnp.dot(span_hot, span_bias.T, precision=lax.Precision.HIGHEST)
    scores = scores + bias.T[:, None, :]
    top = jnp.max(scores, axis=-1, keepdims=True)
    weights = jnp.exp(scores - top)
    total = jnp.sum(weights, axis=-1, keepdims=True)
    values = jnp.einsum(
        "hqk,khd->hqd", weights, k.astype(jnp.float32), precision=lax.Precision.HIGHEST
    )
    return (values / total).transpose(1, 0, 2).reshape(rows, local_width).astype(jnp.bfloat16)


def pair_gather(share):
    other = lax.ppermute(share, "tensor", perm=[(0, 1), (1, 0)])
    low = lax.axis_index("tensor") == 0
    return jnp.concatenate([jnp.where(low, share, other), jnp.where(low, other, share)], axis=0)


def per_device(
    drafts,
    children,
    child_order,
    spans,
    span_bias,
    out_weight,
    norm_gain,
    router,
    routes,
    w_gate,
    w_up,
    w_down,
):
    local_rows, local_width = drafts.shape
    heads_here = span_bias.shape[0]
    head_size = local_width // heads_here
    width = out_weight.shape[1]
    scale = 1.0 / math.sqrt(head_size)
    parents_here = local_rows // R
    leaf_index = lax.axis_index("leaf")
    child_rows = children.shape[0]
    children_here = child_rows // R
    span_rows = -(-spans.shape[0] // local_width)
    span_rows = -(-span_rows // 8) * 8
    span_block = jnp.pad(spans.astype(jnp.bfloat16), (0, span_rows * local_width - spans.shape[0]))
    payload = jnp.concatenate([children, span_block.reshape(span_rows, local_width)], axis=0)
    gathered = lax.all_gather(payload, "leaf", axis=0, tiled=False)
    span_table = gathered[:, child_rows:].reshape(gathered.shape[0], span_rows * local_width)
    count = child_order.shape[0]
    ids = jnp.arange(count, dtype=jnp.int32)
    inverse = jnp.sum(jnp.where(child_order[None, :] == ids[:, None], ids[None, :], 0), axis=1)

    def child_keys(child):
        holder = child // children_here
        offset = (child % children_here) * R
        rows = lax.dynamic_slice(gathered, (holder, offset, 0), (1, R, local_width))[0]
        marks = lax.dynamic_slice(span_table, (holder, offset), (1, R))[0]
        return rows, marks.astype(jnp.int32)

    pieces = []
    for i in range(parents_here):
        parent = leaf_index * parents_here + i
        first_rows, first_spans = child_keys(inverse[2 * parent])
        second_rows, second_spans = child_keys(inverse[2 * parent + 1])
        own_keys = jnp.concatenate([first_rows, second_rows], axis=0)
        own_spans = jnp.concatenate([first_spans, second_spans], axis=0)
        pieces.append(attend_parent(drafts[i * R : (i + 1) * R], own_keys, own_spans, span_bias, scale))
    attended = pieces[0] if parents_here == 1 else jnp.concatenate(pieces, axis=0)
    term = jnp.dot(attended, out_weight, preferred_element_type=jnp.float32)
    offset = lax.axis_index(("expert", "tensor")) * local_width
    own_cols = lax.dynamic_slice(term, (0, offset), (local_rows, local_width)) + drafts.astype(
        jnp.float32
    )
    term = lax.dynamic_update_slice(term, own_cols, (0, offset)).astype(jnp.bfloat16)
    group = lax.axis_size(("expert", "tensor"))
    share_rows = local_rows // group
    arrived_terms = lax.all_to_all(
        term.reshape(group, share_rows, width), ("expert", "tensor"), 0, 0, tiled=True
    )
    share = jnp.sum(arrived_terms.astype(jnp.float32), axis=0)
    merged = pair_gather(share)
    mean_square = jnp.mean(merged * merged, axis=-1, keepdims=True)
    normed = (merged * lax.rsqrt(mean_square + 1e-05) * norm_gain).astype(jnp.bfloat16)
    logits = jnp.dot(normed, router, preferred_element_type=jnp.float32)
    experts = router.shape[1]
    tok_count = routes.shape[0]
    capacity = 4 * tok_count // lax.axis_size("expert")
    choice_hot = routes[:, :, None] == jnp.arange(experts, dtype=jnp.int32)[None, None, :]
    chosen = jnp.sum(jnp.where(choice_hot, logits[:, None, :], 0.0), axis=-1)
    gates = jax.nn.softmax(chosen, axis=-1)
    pairs = routes.reshape(-1)
    pair_hot = (pairs[:, None] == jnp.arange(experts, dtype=jnp.int32)[None, :]).astype(jnp.int32)
    earlier = jnp.cumsum(pair_hot, axis=0) - pair_hot
    slot_index = jnp.sum(earlier * pair_hot, axis=1)
    target = pairs * capacity + slot_index
    place_hot = (
        jnp.arange(experts * capacity, dtype=jnp.int32)[:, None] == target[None, :]
    ).astype(jnp.bfloat16)
    place_rows = jnp.sum(place_hot.reshape(experts * capacity, tok_count, 2), axis=-1)
    outgoing = jnp.dot(place_rows, normed, preferred_element_type=jnp.float32).astype(jnp.bfloat16)
    outgoing = outgoing.reshape(experts, capacity, width)
    chunks = 2
    chunk_slots = capacity // chunks
    returned = []
    for c in range(chunks):
        arrived = lax.all_to_all(
            outgoing[:, c * chunk_slots : (c + 1) * chunk_slots],
            "expert",
            split_axis=0,
            concat_axis=0,
            tiled=True,
        ).reshape(-1, width)
        piece = lax.all_gather(arrived, "leaf", axis=0, tiled=True)
        gate_v = jnp.dot(piece, w_gate[0], preferred_element_type=jnp.float32)
        up_v = jnp.dot(piece, w_up[0], preferred_element_type=jnp.float32)
        hidden = (jax.nn.silu(gate_v) * up_v).astype(jnp.bfloat16)
        down = jnp.dot(hidden, w_down[0], preferred_element_type=jnp.float32).astype(jnp.bfloat16)
        part_rows = lax.psum_scatter(down, "leaf", scatter_dimension=0, tiled=True)
        returned.append(
            lax.all_to_all(
                part_rows.reshape(experts, chunk_slots, width),
                "expert",
                split_axis=0,
                concat_axis=0,
                tiled=True,
            )
        )
    back = jnp.concatenate(returned, axis=1).reshape(-1, width)
    picked = jnp.take(back, target, axis=0)
    other = lax.ppermute(picked, "tensor", perm=[(0, 1), (1, 0)])
    expert_out = (picked.astype(jnp.float32) + other.astype(jnp.float32)).astype(jnp.bfloat16)
    picked = expert_out.astype(jnp.float32).reshape(tok_count, 2, width)
    mixed = gates[:, 0:1] * picked[:, 0] + gates[:, 1:2] * picked[:, 1]
    return merged + mixed


def solution(mesh):
    in_specs = (
        P("leaf", ("expert", "tensor")),
        P("leaf", ("expert", "tensor")),
        P(),
        P("leaf"),
        P(("expert", "tensor"), None),
        P(("expert", "tensor"), None),
        P(),
        P(),
        P(("leaf", "expert"), None),
        P("expert", None, ("leaf", "tensor")),
        P("expert", None, ("leaf", "tensor")),
        P("expert", ("leaf", "tensor"), None),
    )
    out_specs = P(("leaf", "expert"), None)
    return jax.shard_map(
        per_device, mesh=mesh, in_specs=in_specs, out_specs=out_specs, check_vma=False
    )
```

```python
import math

import jax
import jax.numpy as jnp
from jax import lax
from jax.sharding import PartitionSpec as P

R = 256


def attend_parent(queries, keys, key_spans, span_bias, scale):
    rows, local_width = queries.shape
    heads_here, span_count = span_bias.shape
    head_size = local_width // heads_here
    key_count = keys.shape[0]
    q = queries.reshape(rows, heads_here, head_size)
    k = keys.reshape(key_count, heads_here, head_size)
    scores = jnp.einsum("qhd,khd->hqk", q, k, preferred_element_type=jnp.float32) * scale
    span_hot = (key_spans[:, None] == jnp.arange(span_count, dtype=jnp.int32)[None, :]).astype(
        jnp.float32
    )
    bias = jnp.dot(span_hot, span_bias.T, precision=lax.Precision.HIGHEST)
    scores = scores + bias.T[:, None, :]
    top = jnp.max(scores, axis=-1, keepdims=True)
    weights = jnp.exp(scores - top)
    total = jnp.sum(weights, axis=-1, keepdims=True)
    values = jnp.einsum(
        "hqk,khd->hqd", weights, k.astype(jnp.float32), precision=lax.Precision.HIGHEST
    )
    return (values / total).transpose(1, 0, 2).reshape(rows, local_width).astype(jnp.bfloat16)


def pair_gather(share):
    other = lax.ppermute(share, "tensor", perm=[(0, 1), (1, 0)])
    low = lax.axis_index("tensor") == 0
    return jnp.concatenate([jnp.where(low, share, other), jnp.where(low, other, share)], axis=0)


def ring_reduce_leaf(x):
    rows, width = x.shape
    n_leaf = lax.axis_size("leaf")
    n_z = n_leaf // 2
    index = lax.axis_index("leaf")
    core = index % 2
    z = index // 2
    block = rows // n_leaf
    grid = x.reshape(n_z, 2, block, width)
    mine = jnp.where(core == 0, grid[:, 0], grid[:, 1])
    other = jnp.where(core == 0, grid[:, 1], grid[:, 0])
    arrived = lax.ppermute(other, "leaf", perm=[(j, j ^ 1) for j in range(n_leaf)])
    chip = mine.astype(jnp.float32) + arrived.astype(jnp.float32)
    half = width // 2
    east = chip[:, :, :half]
    west = chip[:, :, half:]
    fwd = [(a * 2 + b, ((a + 1) % n_z) * 2 + b) for a in range(n_z) for b in range(2)]
    bwd = [(a * 2 + b, ((a - 1) % n_z) * 2 + b) for a in range(n_z) for b in range(2)]

    def pick(table, at):
        return lax.dynamic_index_in_dim(table, at % n_z, 0, keepdims=False)

    acc_f = pick(east, z - 1)
    acc_b = pick(west, z + 1)
    for step in range(1, n_z):
        got_f = lax.ppermute(acc_f.astype(jnp.bfloat16), "leaf", perm=fwd)
        got_b = lax.ppermute(acc_b.astype(jnp.bfloat16), "leaf", perm=bwd)
        acc_f = got_f.astype(jnp.float32) + pick(east, z - 1 - step)
        acc_b = got_b.astype(jnp.float32) + pick(west, z + 1 + step)
    return jnp.concatenate([acc_f, acc_b], axis=1).astype(jnp.bfloat16)


def per_device(
    drafts,
    children,
    child_order,
    spans,
    span_bias,
    out_weight,
    norm_gain,
    router,
    routes,
    w_gate,
    w_up,
    w_down,
):
    local_rows, local_width = drafts.shape
    heads_here = span_bias.shape[0]
    head_size = local_width // heads_here
    width = out_weight.shape[1]
    scale = 1.0 / math.sqrt(head_size)
    parents_here = local_rows // R
    leaf_index = lax.axis_index("leaf")
    child_rows = children.shape[0]
    children_here = child_rows // R
    span_rows = -(-spans.shape[0] // local_width)
    span_rows = -(-span_rows // 8) * 8
    span_block = jnp.pad(spans.astype(jnp.bfloat16), (0, span_rows * local_width - spans.shape[0]))
    payload = jnp.concatenate([children, span_block.reshape(span_rows, local_width)], axis=0)
    gathered = lax.all_gather(payload, "leaf", axis=0, tiled=False)
    span_table = gathered[:, child_rows:].reshape(gathered.shape[0], span_rows * local_width)
    count = child_order.shape[0]
    ids = jnp.arange(count, dtype=jnp.int32)
    inverse = jnp.sum(jnp.where(child_order[None, :] == ids[:, None], ids[None, :], 0), axis=1)

    def child_keys(child):
        holder = child // children_here
        offset = (child % children_here) * R
        rows = lax.dynamic_slice(gathered, (holder, offset, 0), (1, R, local_width))[0]
        marks = lax.dynamic_slice(span_table, (holder, offset), (1, R))[0]
        return rows, marks.astype(jnp.int32)

    pieces = []
    for i in range(parents_here):
        parent = leaf_index * parents_here + i
        first_rows, first_spans = child_keys(inverse[2 * parent])
        second_rows, second_spans = child_keys(inverse[2 * parent + 1])
        own_keys = jnp.concatenate([first_rows, second_rows], axis=0)
        own_spans = jnp.concatenate([first_spans, second_spans], axis=0)
        pieces.append(attend_parent(drafts[i * R : (i + 1) * R], own_keys, own_spans, span_bias, scale))
    attended = pieces[0] if parents_here == 1 else jnp.concatenate(pieces, axis=0)
    term = jnp.dot(attended, out_weight, preferred_element_type=jnp.float32)
    offset = lax.axis_index(("expert", "tensor")) * local_width
    own_cols = lax.dynamic_slice(term, (0, offset), (local_rows, local_width)) + drafts.astype(
        jnp.float32
    )
    term = lax.dynamic_update_slice(term, own_cols, (0, offset)).astype(jnp.bfloat16)
    group = lax.axis_size(("expert", "tensor"))
    share_rows = local_rows // group
    arrived_terms = lax.all_to_all(
        term.reshape(group, share_rows, width), ("expert", "tensor"), 0, 0, tiled=True
    )
    share = jnp.sum(arrived_terms.astype(jnp.float32), axis=0)
    merged = pair_gather(share)
    mean_square = jnp.mean(merged * merged, axis=-1, keepdims=True)
    normed = (merged * lax.rsqrt(mean_square + 1e-05) * norm_gain).astype(jnp.bfloat16)
    logits = jnp.dot(normed, router, preferred_element_type=jnp.float32)
    experts = router.shape[1]
    tok_count = routes.shape[0]
    capacity = 4 * tok_count // lax.axis_size("expert")
    choice_hot = routes[:, :, None] == jnp.arange(experts, dtype=jnp.int32)[None, None, :]
    chosen = jnp.sum(jnp.where(choice_hot, logits[:, None, :], 0.0), axis=-1)
    gates = jax.nn.softmax(chosen, axis=-1)
    pairs = routes.reshape(-1)
    pair_hot = (pairs[:, None] == jnp.arange(experts, dtype=jnp.int32)[None, :]).astype(jnp.int32)
    earlier = jnp.cumsum(pair_hot, axis=0) - pair_hot
    slot_index = jnp.sum(earlier * pair_hot, axis=1)
    target = pairs * capacity + slot_index
    place_hot = (
        jnp.arange(experts * capacity, dtype=jnp.int32)[:, None] == target[None, :]
    ).astype(jnp.bfloat16)
    place_rows = jnp.sum(place_hot.reshape(experts * capacity, tok_count, 2), axis=-1)
    outgoing = jnp.dot(place_rows, normed, preferred_element_type=jnp.float32).astype(jnp.bfloat16)
    outgoing = outgoing.reshape(experts, capacity, width)
    chunks = 2
    chunk_slots = capacity // chunks
    returned = []
    for c in range(chunks):
        arrived = lax.all_to_all(
            outgoing[:, c * chunk_slots : (c + 1) * chunk_slots],
            "expert",
            split_axis=0,
            concat_axis=0,
            tiled=True,
        ).reshape(-1, width)
        piece = lax.all_gather(arrived, "leaf", axis=0, tiled=True)
        gate_v = jnp.dot(piece, w_gate[0], preferred_element_type=jnp.float32)
        up_v = jnp.dot(piece, w_up[0], preferred_element_type=jnp.float32)
        hidden = (jax.nn.silu(gate_v) * up_v).astype(jnp.bfloat16)
        down = jnp.dot(hidden, w_down[0], preferred_element_type=jnp.float32).astype(jnp.bfloat16)
        if c == 0:
            part_rows = ring_reduce_leaf(down)
        else:
            part_rows = lax.psum_scatter(down, "leaf", scatter_dimension=0, tiled=True)
        returned.append(
            lax.all_to_all(
                part_rows.reshape(experts, chunk_slots, width),
                "expert",
                split_axis=0,
                concat_axis=0,
                tiled=True,
            )
        )
    back = jnp.concatenate(returned, axis=1).reshape(-1, width)
    picked = jnp.take(back, target, axis=0)
    other = lax.ppermute(picked, "tensor", perm=[(0, 1), (1, 0)])
    expert_out = (picked.astype(jnp.float32) + other.astype(jnp.float32)).astype(jnp.bfloat16)
    picked = expert_out.astype(jnp.float32).reshape(tok_count, 2, width)
    mixed = gates[:, 0:1] * picked[:, 0] + gates[:, 1:2] * picked[:, 1]
    return merged + mixed


def solution(mesh):
    in_specs = (
        P("leaf", ("expert", "tensor")),
        P("leaf", ("expert", "tensor")),
        P(),
        P("leaf"),
        P(("expert", "tensor"), None),
        P(("expert", "tensor"), None),
        P(),
        P(),
        P(("leaf", "expert"), None),
        P("expert", None, ("leaf", "tensor")),
        P("expert", None, ("leaf", "tensor")),
        P("expert", ("leaf", "tensor"), None),
    )
    out_specs = P(("leaf", "expert"), None)
    return jax.shard_map(
        per_device, mesh=mesh, in_specs=in_specs, out_specs=out_specs, check_vma=False
    )
```

```python
import math

import jax
import jax.numpy as jnp
from jax import lax
from jax.sharding import PartitionSpec as P

R = 256


def attend_parent(queries, keys, key_spans, span_bias, scale):
    rows, local_width = queries.shape
    heads_here, span_count = span_bias.shape
    head_size = local_width // heads_here
    key_count = keys.shape[0]
    q = queries.reshape(rows, heads_here, head_size)
    k = keys.reshape(key_count, heads_here, head_size)
    scores = jnp.einsum("qhd,khd->hqk", q, k, preferred_element_type=jnp.float32) * scale
    span_hot = (key_spans[:, None] == jnp.arange(span_count, dtype=jnp.int32)[None, :]).astype(
        jnp.float32
    )
    bias = jnp.dot(span_hot, span_bias.T, precision=lax.Precision.HIGHEST)
    scores = scores + bias.T[:, None, :]
    top = jnp.max(scores, axis=-1, keepdims=True)
    weights = jnp.exp(scores - top)
    total = jnp.sum(weights, axis=-1, keepdims=True)
    values = jnp.einsum(
        "hqk,khd->hqd", weights, k.astype(jnp.float32), precision=lax.Precision.HIGHEST
    )
    return (values / total).transpose(1, 0, 2).reshape(rows, local_width).astype(jnp.bfloat16)


def pair_gather(share):
    other = lax.ppermute(share, "tensor", perm=[(0, 1), (1, 0)])
    low = lax.axis_index("tensor") == 0
    return jnp.concatenate([jnp.where(low, share, other), jnp.where(low, other, share)], axis=0)


def per_device(
    drafts,
    children,
    child_order,
    spans,
    span_bias,
    out_weight,
    norm_gain,
    router,
    routes,
    w_gate,
    w_up,
    w_down,
):
    local_rows, local_width = drafts.shape
    heads_here = span_bias.shape[0]
    head_size = local_width // heads_here
    width = out_weight.shape[1]
    scale = 1.0 / math.sqrt(head_size)
    parents_here = local_rows // R
    leaf_index = lax.axis_index("leaf")
    child_rows = children.shape[0]
    children_here = child_rows // R
    span_rows = -(-spans.shape[0] // local_width)
    span_rows = -(-span_rows // 8) * 8
    span_block = jnp.pad(spans.astype(jnp.bfloat16), (0, span_rows * local_width - spans.shape[0]))
    payload = jnp.concatenate([children, span_block.reshape(span_rows, local_width)], axis=0)
    gathered = lax.all_gather(payload, "leaf", axis=0, tiled=False)
    span_table = gathered[:, child_rows:].reshape(gathered.shape[0], span_rows * local_width)
    count = child_order.shape[0]
    ids = jnp.arange(count, dtype=jnp.int32)
    inverse = jnp.sum(jnp.where(child_order[None, :] == ids[:, None], ids[None, :], 0), axis=1)

    def child_keys(child):
        holder = child // children_here
        offset = (child % children_here) * R
        rows = lax.dynamic_slice(gathered, (holder, offset, 0), (1, R, local_width))[0]
        marks = lax.dynamic_slice(span_table, (holder, offset), (1, R))[0]
        return rows, marks.astype(jnp.int32)

    pieces = []
    for i in range(parents_here):
        parent = leaf_index * parents_here + i
        first_rows, first_spans = child_keys(inverse[2 * parent])
        second_rows, second_spans = child_keys(inverse[2 * parent + 1])
        own_keys = jnp.concatenate([first_rows, second_rows], axis=0)
        own_spans = jnp.concatenate([first_spans, second_spans], axis=0)
        pieces.append(attend_parent(drafts[i * R : (i + 1) * R], own_keys, own_spans, span_bias, scale))
    attended = pieces[0] if parents_here == 1 else jnp.concatenate(pieces, axis=0)
    term = jnp.dot(attended, out_weight, preferred_element_type=jnp.float32)
    offset = lax.axis_index(("expert", "tensor")) * local_width
    own_cols = lax.dynamic_slice(term, (0, offset), (local_rows, local_width)) + drafts.astype(
        jnp.float32
    )
    term = lax.dynamic_update_slice(term, own_cols, (0, offset)).astype(jnp.bfloat16)
    group = lax.axis_size(("expert", "tensor"))
    share_rows = local_rows // group
    arrived_terms = lax.all_to_all(
        term.reshape(group, share_rows, width), ("expert", "tensor"), 0, 0, tiled=True
    )
    share = jnp.sum(arrived_terms.astype(jnp.float32), axis=0)
    merged = pair_gather(share)
    mean_square = jnp.mean(merged * merged, axis=-1, keepdims=True)
    normed = (merged * lax.rsqrt(mean_square + 1e-05) * norm_gain).astype(jnp.bfloat16)
    logits = jnp.dot(normed, router, preferred_element_type=jnp.float32)
    experts = router.shape[1]
    tok_count = routes.shape[0]
    capacity = 4 * tok_count // lax.axis_size("expert")
    choice_hot = routes[:, :, None] == jnp.arange(experts, dtype=jnp.int32)[None, None, :]
    chosen = jnp.sum(jnp.where(choice_hot, logits[:, None, :], 0.0), axis=-1)
    gates = jax.nn.softmax(chosen, axis=-1)
    pairs = routes.reshape(-1)
    pair_hot = (pairs[:, None] == jnp.arange(experts, dtype=jnp.int32)[None, :]).astype(jnp.int32)
    earlier = jnp.cumsum(pair_hot, axis=0) - pair_hot
    slot_index = jnp.sum(earlier * pair_hot, axis=1)
    target = pairs * capacity + slot_index
    place_hot = (
        jnp.arange(experts * capacity, dtype=jnp.int32)[:, None] == target[None, :]
    ).astype(jnp.bfloat16)
    place_rows = jnp.sum(place_hot.reshape(experts * capacity, tok_count, 2), axis=-1)
    outgoing = jnp.dot(place_rows, normed, preferred_element_type=jnp.float32).astype(jnp.bfloat16)
    outgoing = outgoing.reshape(experts, capacity, width)
    chunks = 2
    chunk_slots = capacity // chunks
    returned = []
    for c in range(chunks):
        arrived = lax.all_to_all(
            outgoing[:, c * chunk_slots : (c + 1) * chunk_slots],
            "expert",
            split_axis=0,
            concat_axis=0,
            tiled=True,
        ).reshape(-1, width)
        piece = lax.all_gather(arrived, "leaf", axis=0, tiled=True)
        gate_v = jnp.dot(piece, w_gate[0], preferred_element_type=jnp.float32)
        up_v = jnp.dot(piece, w_up[0], preferred_element_type=jnp.float32)
        hidden = (jax.nn.silu(gate_v) * up_v).astype(jnp.bfloat16)
        down = jnp.dot(hidden, w_down[0], preferred_element_type=jnp.float32).astype(jnp.bfloat16)
        part_rows = lax.psum_scatter(down, "leaf", scatter_dimension=0, tiled=True)
        returned.append(
            lax.all_to_all(
                part_rows.reshape(experts, chunk_slots, width),
                "expert",
                split_axis=0,
                concat_axis=0,
                tiled=True,
            )
        )
    back = jnp.concatenate(returned, axis=1).reshape(-1, width)
    picked = jnp.take(back, target, axis=0)
    picked = picked.astype(jnp.float32).reshape(tok_count, 2, width)
    own_mix = (gates[:, 0:1] * picked[:, 0] + gates[:, 1:2] * picked[:, 1]).astype(jnp.bfloat16)
    other_mix = lax.ppermute(own_mix, "tensor", perm=[(0, 1), (1, 0)])
    mixed = own_mix.astype(jnp.float32) + other_mix.astype(jnp.float32)
    return merged + mixed


def solution(mesh):
    in_specs = (
        P("leaf", ("expert", "tensor")),
        P("leaf", ("expert", "tensor")),
        P(),
        P("leaf"),
        P(("expert", "tensor"), None),
        P(("expert", "tensor"), None),
        P(),
        P(),
        P(("leaf", "expert"), None),
        P("expert", None, ("leaf", "tensor")),
        P("expert", None, ("leaf", "tensor")),
        P("expert", ("leaf", "tensor"), None),
    )
    out_specs = P(("leaf", "expert"), None)
    return jax.shard_map(
        per_device, mesh=mesh, in_specs=in_specs, out_specs=out_specs, check_vma=False
    )
```

```python
import math

import jax
import jax.numpy as jnp
from jax import lax
from jax.sharding import PartitionSpec as P

R = 256


def attend_parent(queries, keys, key_spans, span_bias, scale):
    rows, local_width = queries.shape
    heads_here, span_count = span_bias.shape
    head_size = local_width // heads_here
    key_count = keys.shape[0]
    q = queries.reshape(rows, heads_here, head_size)
    k = keys.reshape(key_count, heads_here, head_size)
    scores = jnp.einsum("qhd,khd->hqk", q, k, preferred_element_type=jnp.float32) * scale
    span_hot = (key_spans[:, None] == jnp.arange(span_count, dtype=jnp.int32)[None, :]).astype(
        jnp.float32
    )
    bias = jnp.dot(span_hot, span_bias.T, precision=lax.Precision.HIGHEST)
    scores = scores + bias.T[:, None, :]
    top = jnp.max(scores, axis=-1, keepdims=True)
    weights = jnp.exp(scores - top)
    total = jnp.sum(weights, axis=-1, keepdims=True)
    values = jnp.einsum(
        "hqk,khd->hqd", weights, k.astype(jnp.float32), precision=lax.Precision.HIGHEST
    )
    return (values / total).transpose(1, 0, 2).reshape(rows, local_width).astype(jnp.bfloat16)


def pair_gather(share):
    other = lax.ppermute(share, "tensor", perm=[(0, 1), (1, 0)])
    low = lax.axis_index("tensor") == 0
    return jnp.concatenate([jnp.where(low, share, other), jnp.where(low, other, share)], axis=0)


def per_device(
    drafts,
    children,
    child_order,
    spans,
    span_bias,
    out_weight,
    norm_gain,
    router,
    routes,
    w_gate,
    w_up,
    w_down,
):
    local_rows, local_width = drafts.shape
    heads_here = span_bias.shape[0]
    head_size = local_width // heads_here
    width = out_weight.shape[1]
    scale = 1.0 / math.sqrt(head_size)
    parents_here = local_rows // R
    leaf_index = lax.axis_index("leaf")
    child_rows = children.shape[0]
    children_here = child_rows // R
    span_rows = -(-spans.shape[0] // local_width)
    span_rows = -(-span_rows // 8) * 8
    span_block = jnp.pad(spans.astype(jnp.bfloat16), (0, span_rows * local_width - spans.shape[0]))
    payload = jnp.concatenate([children, span_block.reshape(span_rows, local_width)], axis=0)
    gathered = lax.all_gather(payload, "leaf", axis=0, tiled=False)
    span_table = gathered[:, child_rows:].reshape(gathered.shape[0], span_rows * local_width)
    count = child_order.shape[0]
    ids = jnp.arange(count, dtype=jnp.int32)
    inverse = jnp.sum(jnp.where(child_order[None, :] == ids[:, None], ids[None, :], 0), axis=1)

    def child_keys(child):
        holder = child // children_here
        offset = (child % children_here) * R
        rows = lax.dynamic_slice(gathered, (holder, offset, 0), (1, R, local_width))[0]
        marks = lax.dynamic_slice(span_table, (holder, offset), (1, R))[0]
        return rows, marks.astype(jnp.int32)

    pieces = []
    for i in range(parents_here):
        parent = leaf_index * parents_here + i
        first_rows, first_spans = child_keys(inverse[2 * parent])
        second_rows, second_spans = child_keys(inverse[2 * parent + 1])
        own_keys = jnp.concatenate([first_rows, second_rows], axis=0)
        own_spans = jnp.concatenate([first_spans, second_spans], axis=0)
        pieces.append(attend_parent(drafts[i * R : (i + 1) * R], own_keys, own_spans, span_bias, scale))
    attended = pieces[0] if parents_here == 1 else jnp.concatenate(pieces, axis=0)
    term = jnp.dot(attended, out_weight, preferred_element_type=jnp.float32)
    offset = lax.axis_index(("expert", "tensor")) * local_width
    own_cols = lax.dynamic_slice(term, (0, offset), (local_rows, local_width)) + drafts.astype(
        jnp.float32
    )
    term = lax.dynamic_update_slice(term, own_cols, (0, offset)).astype(jnp.bfloat16)
    group = lax.axis_size(("expert", "tensor"))
    share_rows = local_rows // group
    arrived_terms = lax.all_to_all(
        term.reshape(group, share_rows, width), ("expert", "tensor"), 0, 0, tiled=True
    )
    share = jnp.sum(arrived_terms.astype(jnp.float32), axis=0)
    mean_square = jnp.mean(share * share, axis=-1, keepdims=True)
    normed = pair_gather((share * lax.rsqrt(mean_square + 1e-05) * norm_gain).astype(jnp.bfloat16))
    logits = jnp.dot(normed, router, preferred_element_type=jnp.float32)
    experts = router.shape[1]
    tok_count = routes.shape[0]
    capacity = 4 * tok_count // lax.axis_size("expert")
    choice_hot = routes[:, :, None] == jnp.arange(experts, dtype=jnp.int32)[None, None, :]
    chosen = jnp.sum(jnp.where(choice_hot, logits[:, None, :], 0.0), axis=-1)
    gates = jax.nn.softmax(chosen, axis=-1)
    pairs = routes.reshape(-1)
    pair_hot = (pairs[:, None] == jnp.arange(experts, dtype=jnp.int32)[None, :]).astype(jnp.int32)
    earlier = jnp.cumsum(pair_hot, axis=0) - pair_hot
    slot_index = jnp.sum(earlier * pair_hot, axis=1)
    target = pairs * capacity + slot_index
    place_hot = (
        jnp.arange(experts * capacity, dtype=jnp.int32)[:, None] == target[None, :]
    ).astype(jnp.bfloat16)
    place_rows = jnp.sum(place_hot.reshape(experts * capacity, tok_count, 2), axis=-1)
    outgoing = jnp.dot(place_rows, normed, preferred_element_type=jnp.float32).astype(jnp.bfloat16)
    outgoing = outgoing.reshape(experts, capacity, width)
    chunks = 2
    chunk_slots = capacity // chunks
    returned = []
    for c in range(chunks):
        arrived = lax.all_to_all(
            outgoing[:, c * chunk_slots : (c + 1) * chunk_slots],
            "expert",
            split_axis=0,
            concat_axis=0,
            tiled=True,
        ).reshape(-1, width)
        piece = lax.all_gather(arrived, "leaf", axis=0, tiled=True)
        if c == 0:
            piece, share = lax.optimization_barrier((piece, share))
            other_share = lax.ppermute(share, "tensor", perm=[(0, 1), (1, 0)])
        else:
            piece, other_share = lax.optimization_barrier((piece, other_share))
        gate_v = jnp.dot(piece, w_gate[0], preferred_element_type=jnp.float32)
        up_v = jnp.dot(piece, w_up[0], preferred_element_type=jnp.float32)
        hidden = (jax.nn.silu(gate_v) * up_v).astype(jnp.bfloat16)
        down = jnp.dot(hidden, w_down[0], preferred_element_type=jnp.float32).astype(jnp.bfloat16)
        part_rows = lax.psum_scatter(down, "leaf", scatter_dimension=0, tiled=True)
        returned.append(
            lax.all_to_all(
                part_rows.reshape(experts, chunk_slots, width),
                "expert",
                split_axis=0,
                concat_axis=0,
                tiled=True,
            )
        )
    back = jnp.concatenate(returned, axis=1).reshape(-1, width)
    low = lax.axis_index("tensor") == 0
    merged = jnp.concatenate(
        [jnp.where(low, share, other_share), jnp.where(low, other_share, share)], axis=0
    )
    picked = jnp.take(back, target, axis=0)
    picked = picked.astype(jnp.float32).reshape(tok_count, 2, width)
    own_mix = (gates[:, 0:1] * picked[:, 0] + gates[:, 1:2] * picked[:, 1]).astype(jnp.bfloat16)
    other_mix = lax.ppermute(own_mix, "tensor", perm=[(0, 1), (1, 0)])
    mixed = own_mix.astype(jnp.float32) + other_mix.astype(jnp.float32)
    return merged + mixed


def solution(mesh):
    in_specs = (
        P("leaf", ("expert", "tensor")),
        P("leaf", ("expert", "tensor")),
        P(),
        P("leaf"),
        P(("expert", "tensor"), None),
        P(("expert", "tensor"), None),
        P(),
        P(),
        P(("leaf", "expert"), None),
        P("expert", None, ("leaf", "tensor")),
        P("expert", None, ("leaf", "tensor")),
        P("expert", ("leaf", "tensor"), None),
    )
    out_specs = P(("leaf", "expert"), None)
    return jax.shard_map(
        per_device, mesh=mesh, in_specs=in_specs, out_specs=out_specs, check_vma=False
    )
```

```python
import math

import jax
import jax.numpy as jnp
from jax import lax
from jax.sharding import PartitionSpec as P

R = 256


def attend_parent(queries, keys, key_spans, span_bias, scale):
    rows, local_width = queries.shape
    heads_here, span_count = span_bias.shape
    head_size = local_width // heads_here
    key_count = keys.shape[0]
    q = queries.reshape(rows, heads_here, head_size)
    k = keys.reshape(key_count, heads_here, head_size)
    scores = jnp.einsum("qhd,khd->hqk", q, k, preferred_element_type=jnp.float32) * scale
    span_hot = (key_spans[:, None] == jnp.arange(span_count, dtype=jnp.int32)[None, :]).astype(
        jnp.float32
    )
    bias = jnp.dot(span_hot, span_bias.T, precision=lax.Precision.HIGHEST)
    scores = scores + bias.T[:, None, :]
    top = jnp.max(scores, axis=-1, keepdims=True)
    weights = jnp.exp(scores - top)
    total = jnp.sum(weights, axis=-1, keepdims=True)
    values = jnp.einsum(
        "hqk,khd->hqd", weights, k.astype(jnp.float32), precision=lax.Precision.HIGHEST
    )
    return (values / total).transpose(1, 0, 2).reshape(rows, local_width).astype(jnp.bfloat16)


def pair_gather(share):
    other = lax.ppermute(share, "tensor", perm=[(0, 1), (1, 0)])
    low = lax.axis_index("tensor") == 0
    return jnp.concatenate([jnp.where(low, share, other), jnp.where(low, other, share)], axis=0)


def per_device(
    drafts,
    children,
    child_order,
    spans,
    span_bias,
    out_weight,
    norm_gain,
    router,
    routes,
    w_gate,
    w_up,
    w_down,
):
    local_rows, local_width = drafts.shape
    heads_here = span_bias.shape[0]
    head_size = local_width // heads_here
    width = out_weight.shape[1]
    scale = 1.0 / math.sqrt(head_size)
    parents_here = local_rows // R
    leaf_index = lax.axis_index("leaf")
    child_rows = children.shape[0]
    children_here = child_rows // R
    span_rows = -(-spans.shape[0] // local_width)
    span_rows = -(-span_rows // 8) * 8
    span_block = jnp.pad(spans.astype(jnp.bfloat16), (0, span_rows * local_width - spans.shape[0]))
    payload = jnp.concatenate([children, span_block.reshape(span_rows, local_width)], axis=0)
    gathered = lax.all_gather(payload, "leaf", axis=0, tiled=False)
    span_table = gathered[:, child_rows:].reshape(gathered.shape[0], span_rows * local_width)
    count = child_order.shape[0]
    ids = jnp.arange(count, dtype=jnp.int32)
    inverse = jnp.sum(jnp.where(child_order[None, :] == ids[:, None], ids[None, :], 0), axis=1)

    def child_keys(child):
        holder = child // children_here
        offset = (child % children_here) * R
        rows = lax.dynamic_slice(gathered, (holder, offset, 0), (1, R, local_width))[0]
        marks = lax.dynamic_slice(span_table, (holder, offset), (1, R))[0]
        return rows, marks.astype(jnp.int32)

    pieces = []
    for i in range(parents_here):
        parent = leaf_index * parents_here + i
        first_rows, first_spans = child_keys(inverse[2 * parent])
        second_rows, second_spans = child_keys(inverse[2 * parent + 1])
        own_keys = jnp.concatenate([first_rows, second_rows], axis=0)
        own_spans = jnp.concatenate([first_spans, second_spans], axis=0)
        pieces.append(attend_parent(drafts[i * R : (i + 1) * R], own_keys, own_spans, span_bias, scale))
    attended = pieces[0] if parents_here == 1 else jnp.concatenate(pieces, axis=0)
    term = jnp.dot(attended, out_weight, preferred_element_type=jnp.float32)
    offset = lax.axis_index(("expert", "tensor")) * local_width
    own_cols = lax.dynamic_slice(term, (0, offset), (local_rows, local_width)) + drafts.astype(
        jnp.float32
    )
    term = lax.dynamic_update_slice(term, own_cols, (0, offset)).astype(jnp.bfloat16)
    group = lax.axis_size("expert")
    group_rows = local_rows // group
    arrived_terms = lax.all_to_all(
        term.reshape(group, group_rows, width), "expert", 0, 0, tiled=True
    )
    pair_sum = jnp.sum(arrived_terms.astype(jnp.float32), axis=0)
    half = group_rows // 2
    low = lax.axis_index("tensor") == 0
    mine = jnp.where(low, pair_sum[:half], pair_sum[half:])
    theirs = jnp.where(low, pair_sum[half:], pair_sum[:half])
    share = mine + lax.ppermute(theirs, "tensor", perm=[(0, 1), (1, 0)])
    mean_square = jnp.mean(share * share, axis=-1, keepdims=True)
    normed = pair_gather((share * lax.rsqrt(mean_square + 1e-05) * norm_gain).astype(jnp.bfloat16))
    logits = jnp.dot(normed, router, preferred_element_type=jnp.float32)
    experts = router.shape[1]
    tok_count = routes.shape[0]
    capacity = 4 * tok_count // lax.axis_size("expert")
    choice_hot = routes[:, :, None] == jnp.arange(experts, dtype=jnp.int32)[None, None, :]
    chosen = jnp.sum(jnp.where(choice_hot, logits[:, None, :], 0.0), axis=-1)
    gates = jax.nn.softmax(chosen, axis=-1)
    pairs = routes.reshape(-1)
    pair_hot = (pairs[:, None] == jnp.arange(experts, dtype=jnp.int32)[None, :]).astype(jnp.int32)
    earlier = jnp.cumsum(pair_hot, axis=0) - pair_hot
    slot_index = jnp.sum(earlier * pair_hot, axis=1)
    target = pairs * capacity + slot_index
    place_hot = (
        jnp.arange(experts * capacity, dtype=jnp.int32)[:, None] == target[None, :]
    ).astype(jnp.bfloat16)
    place_rows = jnp.sum(place_hot.reshape(experts * capacity, tok_count, 2), axis=-1)
    outgoing = jnp.dot(place_rows, normed, preferred_element_type=jnp.float32).astype(jnp.bfloat16)
    outgoing = outgoing.reshape(experts, capacity, width)
    chunks = 2
    chunk_slots = capacity // chunks
    returned = []
    for c in range(chunks):
        arrived = lax.all_to_all(
            outgoing[:, c * chunk_slots : (c + 1) * chunk_slots],
            "expert",
            split_axis=0,
            concat_axis=0,
            tiled=True,
        ).reshape(-1, width)
        piece = lax.all_gather(arrived, "leaf", axis=0, tiled=True)
        if c == 0:
            piece, share = lax.optimization_barrier((piece, share))
            other_share = lax.ppermute(share, "tensor", perm=[(0, 1), (1, 0)])
        else:
            piece, other_share = lax.optimization_barrier((piece, other_share))
        gate_v = jnp.dot(piece, w_gate[0], preferred_element_type=jnp.float32)
        up_v = jnp.dot(piece, w_up[0], preferred_element_type=jnp.float32)
        hidden = (jax.nn.silu(gate_v) * up_v).astype(jnp.bfloat16)
        down = jnp.dot(hidden, w_down[0], preferred_element_type=jnp.float32).astype(jnp.bfloat16)
        part_rows = lax.psum_scatter(down, "leaf", scatter_dimension=0, tiled=True)
        returned.append(
            lax.all_to_all(
                part_rows.reshape(experts, chunk_slots, width),
                "expert",
                split_axis=0,
                concat_axis=0,
                tiled=True,
            )
        )
    back = jnp.concatenate(returned, axis=1).reshape(-1, width)
    low = lax.axis_index("tensor") == 0
    merged = jnp.concatenate(
        [jnp.where(low, share, other_share), jnp.where(low, other_share, share)], axis=0
    )
    picked = jnp.take(back, target, axis=0)
    picked = picked.astype(jnp.float32).reshape(tok_count, 2, width)
    own_mix = (gates[:, 0:1] * picked[:, 0] + gates[:, 1:2] * picked[:, 1]).astype(jnp.bfloat16)
    other_mix = lax.ppermute(own_mix, "tensor", perm=[(0, 1), (1, 0)])
    mixed = own_mix.astype(jnp.float32) + other_mix.astype(jnp.float32)
    return merged + mixed


def solution(mesh):
    in_specs = (
        P("leaf", ("expert", "tensor")),
        P("leaf", ("expert", "tensor")),
        P(),
        P("leaf"),
        P(("expert", "tensor"), None),
        P(("expert", "tensor"), None),
        P(),
        P(),
        P(("leaf", "expert"), None),
        P("expert", None, ("leaf", "tensor")),
        P("expert", None, ("leaf", "tensor")),
        P("expert", ("leaf", "tensor"), None),
    )
    out_specs = P(("leaf", "expert"), None)
    return jax.shard_map(
        per_device, mesh=mesh, in_specs=in_specs, out_specs=out_specs, check_vma=False
    )
```

```python
import math

import jax
import jax.numpy as jnp
from jax import lax
from jax.sharding import PartitionSpec as P

R = 256


def attend_parent(queries, keys, key_spans, span_bias, scale):
    rows, local_width = queries.shape
    heads_here, span_count = span_bias.shape
    head_size = local_width // heads_here
    key_count = keys.shape[0]
    q = queries.reshape(rows, heads_here, head_size)
    k = keys.reshape(key_count, heads_here, head_size)
    scores = jnp.einsum("qhd,khd->hqk", q, k, preferred_element_type=jnp.float32) * scale
    span_hot = (key_spans[:, None] == jnp.arange(span_count, dtype=jnp.int32)[None, :]).astype(
        jnp.float32
    )
    bias = jnp.dot(span_hot, span_bias.T, precision=lax.Precision.HIGHEST)
    scores = scores + bias.T[:, None, :]
    top = jnp.max(scores, axis=-1, keepdims=True)
    weights = jnp.exp(scores - top)
    total = jnp.sum(weights, axis=-1, keepdims=True)
    values = jnp.einsum(
        "hqk,khd->hqd", weights, k.astype(jnp.float32), precision=lax.Precision.HIGHEST
    )
    return (values / total).transpose(1, 0, 2).reshape(rows, local_width).astype(jnp.bfloat16)


def pair_gather(share):
    other = lax.ppermute(share, "tensor", perm=[(0, 1), (1, 0)])
    low = lax.axis_index("tensor") == 0
    return jnp.concatenate([jnp.where(low, share, other), jnp.where(low, other, share)], axis=0)


def gather_leaf(x):
    rows, width = x.shape
    n_leaf = lax.axis_size("leaf")
    n_z = n_leaf // 2
    index = lax.axis_index("leaf")
    core = index % 2
    z = index // 2
    got = [x]
    for k in range(1, n_z):
        perm = [(a * 2 + b, ((a + k) % n_z) * 2 + b) for a in range(n_z) for b in range(2)]
        got.append(lax.ppermute(x, "leaf", perm=perm))
    mine = jnp.stack(got)
    other = lax.ppermute(mine, "leaf", perm=[(j, j ^ 1) for j in range(n_leaf)])
    both = jnp.concatenate([mine, other], axis=0)
    zz = jnp.arange(n_z, dtype=jnp.int32)[:, None]
    cc = jnp.arange(2, dtype=jnp.int32)[None, :]
    order = jnp.where(cc == core, 0, n_z) + (z - zz) % n_z
    return jnp.take(both, order.reshape(-1), axis=0).reshape(n_leaf * rows, width)


def per_device(
    drafts,
    children,
    child_order,
    spans,
    span_bias,
    out_weight,
    norm_gain,
    router,
    routes,
    w_gate,
    w_up,
    w_down,
):
    local_rows, local_width = drafts.shape
    heads_here = span_bias.shape[0]
    head_size = local_width // heads_here
    width = out_weight.shape[1]
    scale = 1.0 / math.sqrt(head_size)
    parents_here = local_rows // R
    leaf_index = lax.axis_index("leaf")
    child_rows = children.shape[0]
    children_here = child_rows // R
    span_rows = -(-spans.shape[0] // local_width)
    span_rows = -(-span_rows // 8) * 8
    span_block = jnp.pad(spans.astype(jnp.bfloat16), (0, span_rows * local_width - spans.shape[0]))
    payload = jnp.concatenate([children, span_block.reshape(span_rows, local_width)], axis=0)
    gathered = lax.all_gather(payload, "leaf", axis=0, tiled=False)
    span_table = gathered[:, child_rows:].reshape(gathered.shape[0], span_rows * local_width)
    count = child_order.shape[0]
    ids = jnp.arange(count, dtype=jnp.int32)
    inverse = jnp.sum(jnp.where(child_order[None, :] == ids[:, None], ids[None, :], 0), axis=1)

    def child_keys(child):
        holder = child // children_here
        offset = (child % children_here) * R
        rows = lax.dynamic_slice(gathered, (holder, offset, 0), (1, R, local_width))[0]
        marks = lax.dynamic_slice(span_table, (holder, offset), (1, R))[0]
        return rows, marks.astype(jnp.int32)

    pieces = []
    for i in range(parents_here):
        parent = leaf_index * parents_here + i
        first_rows, first_spans = child_keys(inverse[2 * parent])
        second_rows, second_spans = child_keys(inverse[2 * parent + 1])
        own_keys = jnp.concatenate([first_rows, second_rows], axis=0)
        own_spans = jnp.concatenate([first_spans, second_spans], axis=0)
        pieces.append(attend_parent(drafts[i * R : (i + 1) * R], own_keys, own_spans, span_bias, scale))
    attended = pieces[0] if parents_here == 1 else jnp.concatenate(pieces, axis=0)
    term = jnp.dot(attended, out_weight, preferred_element_type=jnp.float32)
    offset = lax.axis_index(("expert", "tensor")) * local_width
    own_cols = lax.dynamic_slice(term, (0, offset), (local_rows, local_width)) + drafts.astype(
        jnp.float32
    )
    term = lax.dynamic_update_slice(term, own_cols, (0, offset)).astype(jnp.bfloat16)
    group = lax.axis_size(("expert", "tensor"))
    share_rows = local_rows // group
    arrived_terms = lax.all_to_all(
        term.reshape(group, share_rows, width), ("expert", "tensor"), 0, 0, tiled=True
    )
    share = jnp.sum(arrived_terms.astype(jnp.float32), axis=0)
    mean_square = jnp.mean(share * share, axis=-1, keepdims=True)
    normed = pair_gather((share * lax.rsqrt(mean_square + 1e-05) * norm_gain).astype(jnp.bfloat16))
    logits = jnp.dot(normed, router, preferred_element_type=jnp.float32)
    experts = router.shape[1]
    tok_count = routes.shape[0]
    capacity = 4 * tok_count // lax.axis_size("expert")
    choice_hot = routes[:, :, None] == jnp.arange(experts, dtype=jnp.int32)[None, None, :]
    chosen = jnp.sum(jnp.where(choice_hot, logits[:, None, :], 0.0), axis=-1)
    gates = jax.nn.softmax(chosen, axis=-1)
    pairs = routes.reshape(-1)
    pair_hot = (pairs[:, None] == jnp.arange(experts, dtype=jnp.int32)[None, :]).astype(jnp.int32)
    earlier = jnp.cumsum(pair_hot, axis=0) - pair_hot
    slot_index = jnp.sum(earlier * pair_hot, axis=1)
    target = pairs * capacity + slot_index
    place_hot = (
        jnp.arange(experts * capacity, dtype=jnp.int32)[:, None] == target[None, :]
    ).astype(jnp.bfloat16)
    place_rows = jnp.sum(place_hot.reshape(experts * capacity, tok_count, 2), axis=-1)
    outgoing = jnp.dot(place_rows, normed, preferred_element_type=jnp.float32).astype(jnp.bfloat16)
    outgoing = outgoing.reshape(experts, capacity, width)
    chunks = 2
    chunk_slots = capacity // chunks
    returned = []
    for c in range(chunks):
        arrived = lax.all_to_all(
            outgoing[:, c * chunk_slots : (c + 1) * chunk_slots],
            "expert",
            split_axis=0,
            concat_axis=0,
            tiled=True,
        ).reshape(-1, width)
        piece = gather_leaf(arrived)
        if c == 0:
            piece, share = lax.optimization_barrier((piece, share))
            other_share = lax.ppermute(share, "tensor", perm=[(0, 1), (1, 0)])
        else:
            piece, other_share = lax.optimization_barrier((piece, other_share))
        gate_v = jnp.dot(piece, w_gate[0], preferred_element_type=jnp.float32)
        up_v = jnp.dot(piece, w_up[0], preferred_element_type=jnp.float32)
        hidden = (jax.nn.silu(gate_v) * up_v).astype(jnp.bfloat16)
        down = jnp.dot(hidden, w_down[0], preferred_element_type=jnp.float32).astype(jnp.bfloat16)
        part_rows = lax.psum_scatter(down, "leaf", scatter_dimension=0, tiled=True)
        returned.append(
            lax.all_to_all(
                part_rows.reshape(experts, chunk_slots, width),
                "expert",
                split_axis=0,
                concat_axis=0,
                tiled=True,
            )
        )
    back = jnp.concatenate(returned, axis=1).reshape(-1, width)
    low = lax.axis_index("tensor") == 0
    merged = jnp.concatenate(
        [jnp.where(low, share, other_share), jnp.where(low, other_share, share)], axis=0
    )
    picked = jnp.take(back, target, axis=0)
    picked = picked.astype(jnp.float32).reshape(tok_count, 2, width)
    own_mix = (gates[:, 0:1] * picked[:, 0] + gates[:, 1:2] * picked[:, 1]).astype(jnp.bfloat16)
    other_mix = lax.ppermute(own_mix, "tensor", perm=[(0, 1), (1, 0)])
    mixed = own_mix.astype(jnp.float32) + other_mix.astype(jnp.float32)
    return merged + mixed


def solution(mesh):
    in_specs = (
        P("leaf", ("expert", "tensor")),
        P("leaf", ("expert", "tensor")),
        P(),
        P("leaf"),
        P(("expert", "tensor"), None),
        P(("expert", "tensor"), None),
        P(),
        P(),
        P(("leaf", "expert"), None),
        P("expert", None, ("leaf", "tensor")),
        P("expert", None, ("leaf", "tensor")),
        P("expert", ("leaf", "tensor"), None),
    )
    out_specs = P(("leaf", "expert"), None)
    return jax.shard_map(
        per_device, mesh=mesh, in_specs=in_specs, out_specs=out_specs, check_vma=False
    )
```

```python
import math

import jax
import jax.numpy as jnp
from jax import lax
from jax.sharding import PartitionSpec as P

R = 256


def attend_parent(queries, keys, key_spans, span_bias, scale):
    rows, local_width = queries.shape
    heads_here, span_count = span_bias.shape
    head_size = local_width // heads_here
    key_count = keys.shape[0]
    q = queries.reshape(rows, heads_here, head_size)
    k = keys.reshape(key_count, heads_here, head_size)
    scores = jnp.einsum("qhd,khd->hqk", q, k, preferred_element_type=jnp.float32) * scale
    span_hot = (key_spans[:, None] == jnp.arange(span_count, dtype=jnp.int32)[None, :]).astype(
        jnp.float32
    )
    bias = jnp.dot(span_hot, span_bias.T, precision=lax.Precision.HIGHEST)
    scores = scores + bias.T[:, None, :]
    top = jnp.max(scores, axis=-1, keepdims=True)
    weights = jnp.exp(scores - top)
    total = jnp.sum(weights, axis=-1, keepdims=True)
    values = jnp.einsum(
        "hqk,khd->hqd", weights, k.astype(jnp.float32), precision=lax.Precision.HIGHEST
    )
    return (values / total).transpose(1, 0, 2).reshape(rows, local_width).astype(jnp.bfloat16)


def pair_gather(share):
    other = lax.ppermute(share, "tensor", perm=[(0, 1), (1, 0)])
    low = lax.axis_index("tensor") == 0
    return jnp.concatenate([jnp.where(low, share, other), jnp.where(low, other, share)], axis=0)


def per_device(
    drafts,
    children,
    child_order,
    spans,
    span_bias,
    out_weight,
    norm_gain,
    router,
    routes,
    w_gate,
    w_up,
    w_down,
):
    local_rows, local_width = drafts.shape
    heads_here = span_bias.shape[0]
    head_size = local_width // heads_here
    width = out_weight.shape[1]
    scale = 1.0 / math.sqrt(head_size)
    parents_here = local_rows // R
    leaf_index = lax.axis_index("leaf")
    child_rows = children.shape[0]
    children_here = child_rows // R
    span_rows = -(-spans.shape[0] // local_width)
    span_rows = -(-span_rows // 8) * 8
    span_block = jnp.pad(spans.astype(jnp.bfloat16), (0, span_rows * local_width - spans.shape[0]))
    payload = jnp.concatenate([children, span_block.reshape(span_rows, local_width)], axis=0)
    n_leaf = lax.axis_size("leaf")
    n_z = n_leaf // 2
    core = leaf_index % 2
    z = leaf_index // 2
    got = [payload]
    for k in range(1, n_z):
        perm = [(a * 2 + b, ((a + k) % n_z) * 2 + b) for a in range(n_z) for b in range(2)]
        got.append(lax.ppermute(payload, "leaf", perm=perm))
    swap = [(j, j ^ 1) for j in range(n_leaf)]
    got = got + [lax.ppermute(block, "leaf", perm=swap) for block in got]
    gathered = jnp.stack(got)
    span_table = gathered[:, child_rows:].reshape(gathered.shape[0], span_rows * local_width)
    count = child_order.shape[0]
    ids = jnp.arange(count, dtype=jnp.int32)
    inverse = jnp.sum(jnp.where(child_order[None, :] == ids[:, None], ids[None, :], 0), axis=1)

    def child_keys(child):
        owner = child // children_here
        slot = jnp.where(owner % 2 == core, 0, n_z) + (z - owner // 2) % n_z
        offset = (child % children_here) * R
        rows = lax.dynamic_slice(gathered, (slot, offset, 0), (1, R, local_width))[0]
        marks = lax.dynamic_slice(span_table, (slot, offset), (1, R))[0]
        return rows, marks.astype(jnp.int32)

    pieces = []
    for i in range(parents_here):
        parent = leaf_index * parents_here + i
        first_rows, first_spans = child_keys(inverse[2 * parent])
        second_rows, second_spans = child_keys(inverse[2 * parent + 1])
        own_keys = jnp.concatenate([first_rows, second_rows], axis=0)
        own_spans = jnp.concatenate([first_spans, second_spans], axis=0)
        pieces.append(attend_parent(drafts[i * R : (i + 1) * R], own_keys, own_spans, span_bias, scale))
    attended = pieces[0] if parents_here == 1 else jnp.concatenate(pieces, axis=0)
    term = jnp.dot(attended, out_weight, preferred_element_type=jnp.float32)
    offset = lax.axis_index(("expert", "tensor")) * local_width
    own_cols = lax.dynamic_slice(term, (0, offset), (local_rows, local_width)) + drafts.astype(
        jnp.float32
    )
    term = lax.dynamic_update_slice(term, own_cols, (0, offset)).astype(jnp.bfloat16)
    group = lax.axis_size(("expert", "tensor"))
    share_rows = local_rows // group
    arrived_terms = lax.all_to_all(
        term.reshape(group, share_rows, width), ("expert", "tensor"), 0, 0, tiled=True
    )
    share = jnp.sum(arrived_terms.astype(jnp.float32), axis=0)
    mean_square = jnp.mean(share * share, axis=-1, keepdims=True)
    normed = pair_gather((share * lax.rsqrt(mean_square + 1e-05) * norm_gain).astype(jnp.bfloat16))
    logits = jnp.dot(normed, router, preferred_element_type=jnp.float32)
    experts = router.shape[1]
    tok_count = routes.shape[0]
    capacity = 4 * tok_count // lax.axis_size("expert")
    choice_hot = routes[:, :, None] == jnp.arange(experts, dtype=jnp.int32)[None, None, :]
    chosen = jnp.sum(jnp.where(choice_hot, logits[:, None, :], 0.0), axis=-1)
    gates = jax.nn.softmax(chosen, axis=-1)
    pairs = routes.reshape(-1)
    pair_hot = (pairs[:, None] == jnp.arange(experts, dtype=jnp.int32)[None, :]).astype(jnp.int32)
    earlier = jnp.cumsum(pair_hot, axis=0) - pair_hot
    slot_index = jnp.sum(earlier * pair_hot, axis=1)
    target = pairs * capacity + slot_index
    place_hot = (
        jnp.arange(experts * capacity, dtype=jnp.int32)[:, None] == target[None, :]
    ).astype(jnp.bfloat16)
    place_rows = jnp.sum(place_hot.reshape(experts * capacity, tok_count, 2), axis=-1)
    outgoing = jnp.dot(place_rows, normed, preferred_element_type=jnp.float32).astype(jnp.bfloat16)
    outgoing = outgoing.reshape(experts, capacity, width)
    chunks = 2
    chunk_slots = capacity // chunks
    returned = []
    for c in range(chunks):
        arrived = lax.all_to_all(
            outgoing[:, c * chunk_slots : (c + 1) * chunk_slots],
            "expert",
            split_axis=0,
            concat_axis=0,
            tiled=True,
        ).reshape(-1, width)
        piece = lax.all_gather(arrived, "leaf", axis=0, tiled=True)
        if c == 0:
            piece, share = lax.optimization_barrier((piece, share))
            other_share = lax.ppermute(share, "tensor", perm=[(0, 1), (1, 0)])
        else:
            piece, other_share = lax.optimization_barrier((piece, other_share))
        gate_v = jnp.dot(piece, w_gate[0], preferred_element_type=jnp.float32)
        up_v = jnp.dot(piece, w_up[0], preferred_element_type=jnp.float32)
        hidden = (jax.nn.silu(gate_v) * up_v).astype(jnp.bfloat16)
        down = jnp.dot(hidden, w_down[0], preferred_element_type=jnp.float32).astype(jnp.bfloat16)
        part_rows = lax.psum_scatter(down, "leaf", scatter_dimension=0, tiled=True)
        returned.append(
            lax.all_to_all(
                part_rows.reshape(experts, chunk_slots, width),
                "expert",
                split_axis=0,
                concat_axis=0,
                tiled=True,
            )
        )
    back = jnp.concatenate(returned, axis=1).reshape(-1, width)
    low = lax.axis_index("tensor") == 0
    merged = jnp.concatenate(
        [jnp.where(low, share, other_share), jnp.where(low, other_share, share)], axis=0
    )
    picked = jnp.take(back, target, axis=0)
    picked = picked.astype(jnp.float32).reshape(tok_count, 2, width)
    own_mix = (gates[:, 0:1] * picked[:, 0] + gates[:, 1:2] * picked[:, 1]).astype(jnp.bfloat16)
    other_mix = lax.ppermute(own_mix, "tensor", perm=[(0, 1), (1, 0)])
    mixed = own_mix.astype(jnp.float32) + other_mix.astype(jnp.float32)
    return merged + mixed


def solution(mesh):
    in_specs = (
        P("leaf", ("expert", "tensor")),
        P("leaf", ("expert", "tensor")),
        P(),
        P("leaf"),
        P(("expert", "tensor"), None),
        P(("expert", "tensor"), None),
        P(),
        P(),
        P(("leaf", "expert"), None),
        P("expert", None, ("leaf", "tensor")),
        P("expert", None, ("leaf", "tensor")),
        P("expert", ("leaf", "tensor"), None),
    )
    out_specs = P(("leaf", "expert"), None)
    return jax.shard_map(
        per_device, mesh=mesh, in_specs=in_specs, out_specs=out_specs, check_vma=False
    )
```

```python
import math

import jax
import jax.numpy as jnp
from jax import lax
from jax.sharding import PartitionSpec as P

R = 256


def attend_parent(queries, keys, key_spans, span_bias, scale):
    rows, local_width = queries.shape
    heads_here, span_count = span_bias.shape
    head_size = local_width // heads_here
    key_count = keys.shape[0]
    q = queries.reshape(rows, heads_here, head_size)
    k = keys.reshape(key_count, heads_here, head_size)
    scores = jnp.einsum("qhd,khd->hqk", q, k, preferred_element_type=jnp.float32) * scale
    span_hot = (key_spans[:, None] == jnp.arange(span_count, dtype=jnp.int32)[None, :]).astype(
        jnp.float32
    )
    bias = jnp.dot(span_hot, span_bias.T, precision=lax.Precision.HIGHEST)
    scores = scores + bias.T[:, None, :]
    top = jnp.max(scores, axis=-1, keepdims=True)
    weights = jnp.exp(scores - top)
    total = jnp.sum(weights, axis=-1, keepdims=True)
    values = jnp.einsum(
        "hqk,khd->hqd", weights, k.astype(jnp.float32), precision=lax.Precision.HIGHEST
    )
    return (values / total).transpose(1, 0, 2).reshape(rows, local_width).astype(jnp.bfloat16)


def pair_gather(share):
    other = lax.ppermute(share, "tensor", perm=[(0, 1), (1, 0)])
    low = lax.axis_index("tensor") == 0
    return jnp.concatenate([jnp.where(low, share, other), jnp.where(low, other, share)], axis=0)


def leaf_spread(x):
    n_leaf = lax.axis_size("leaf")
    n_z = n_leaf // 2
    got = [x]
    for k in range(1, n_z):
        perm = [(a * 2 + b, ((a + k) % n_z) * 2 + b) for a in range(n_z) for b in range(2)]
        got.append(lax.ppermute(x, "leaf", perm=perm))
    swap = [(j, j ^ 1) for j in range(n_leaf)]
    return got + [lax.ppermute(block, "leaf", perm=swap) for block in got]


def leaf_order():
    n_leaf = lax.axis_size("leaf")
    n_z = n_leaf // 2
    index = lax.axis_index("leaf")
    owner = jnp.arange(n_leaf, dtype=jnp.int32)
    return jnp.where(owner % 2 == index % 2, 0, n_z) + (index // 2 - owner // 2) % n_z


def per_device(
    drafts,
    children,
    child_order,
    spans,
    span_bias,
    out_weight,
    norm_gain,
    router,
    routes,
    w_gate,
    w_up,
    w_down,
):
    local_rows, local_width = drafts.shape
    heads_here = span_bias.shape[0]
    head_size = local_width // heads_here
    width = out_weight.shape[1]
    scale = 1.0 / math.sqrt(head_size)
    parents_here = local_rows // R
    leaf_index = lax.axis_index("leaf")
    child_rows = children.shape[0]
    children_here = child_rows // R
    span_rows = -(-spans.shape[0] // local_width)
    span_rows = -(-span_rows // 8) * 8
    span_block = jnp.pad(spans.astype(jnp.bfloat16), (0, span_rows * local_width - spans.shape[0]))
    payload = jnp.concatenate([children, span_block.reshape(span_rows, local_width)], axis=0)
    n_leaf = lax.axis_size("leaf")
    n_z = n_leaf // 2
    core = leaf_index % 2
    z = leaf_index // 2
    got = [payload]
    for k in range(1, n_z):
        perm = [(a * 2 + b, ((a + k) % n_z) * 2 + b) for a in range(n_z) for b in range(2)]
        got.append(lax.ppermute(payload, "leaf", perm=perm))
    swap = [(j, j ^ 1) for j in range(n_leaf)]
    got = got + [lax.ppermute(block, "leaf", perm=swap) for block in got]
    gathered = jnp.stack(got)
    span_table = gathered[:, child_rows:].reshape(gathered.shape[0], span_rows * local_width)
    count = child_order.shape[0]
    ids = jnp.arange(count, dtype=jnp.int32)
    inverse = jnp.sum(jnp.where(child_order[None, :] == ids[:, None], ids[None, :], 0), axis=1)

    def child_keys(child):
        owner = child // children_here
        slot = jnp.where(owner % 2 == core, 0, n_z) + (z - owner // 2) % n_z
        offset = (child % children_here) * R
        rows = lax.dynamic_slice(gathered, (slot, offset, 0), (1, R, local_width))[0]
        marks = lax.dynamic_slice(span_table, (slot, offset), (1, R))[0]
        return rows, marks.astype(jnp.int32)

    pieces = []
    for i in range(parents_here):
        parent = leaf_index * parents_here + i
        first_rows, first_spans = child_keys(inverse[2 * parent])
        second_rows, second_spans = child_keys(inverse[2 * parent + 1])
        own_keys = jnp.concatenate([first_rows, second_rows], axis=0)
        own_spans = jnp.concatenate([first_spans, second_spans], axis=0)
        pieces.append(attend_parent(drafts[i * R : (i + 1) * R], own_keys, own_spans, span_bias, scale))
    attended = pieces[0] if parents_here == 1 else jnp.concatenate(pieces, axis=0)
    term = jnp.dot(attended, out_weight, preferred_element_type=jnp.float32)
    offset = lax.axis_index(("expert", "tensor")) * local_width
    own_cols = lax.dynamic_slice(term, (0, offset), (local_rows, local_width)) + drafts.astype(
        jnp.float32
    )
    term = lax.dynamic_update_slice(term, own_cols, (0, offset)).astype(jnp.bfloat16)
    group = lax.axis_size(("expert", "tensor"))
    share_rows = local_rows // group
    arrived_terms = lax.all_to_all(
        term.reshape(group, share_rows, width), ("expert", "tensor"), 0, 0, tiled=True
    )
    share = jnp.sum(arrived_terms.astype(jnp.float32), axis=0)
    mean_square = jnp.mean(share * share, axis=-1, keepdims=True)
    normed = pair_gather((share * lax.rsqrt(mean_square + 1e-05) * norm_gain).astype(jnp.bfloat16))
    logits = jnp.dot(normed, router, preferred_element_type=jnp.float32)
    experts = router.shape[1]
    tok_count = routes.shape[0]
    capacity = 4 * tok_count // lax.axis_size("expert")
    choice_hot = routes[:, :, None] == jnp.arange(experts, dtype=jnp.int32)[None, None, :]
    chosen = jnp.sum(jnp.where(choice_hot, logits[:, None, :], 0.0), axis=-1)
    gates = jax.nn.softmax(chosen, axis=-1)
    pairs = routes.reshape(-1)
    pair_hot = (pairs[:, None] == jnp.arange(experts, dtype=jnp.int32)[None, :]).astype(jnp.int32)
    earlier = jnp.cumsum(pair_hot, axis=0) - pair_hot
    slot_index = jnp.sum(earlier * pair_hot, axis=1)
    target = pairs * capacity + slot_index
    place_hot = (
        jnp.arange(experts * capacity, dtype=jnp.int32)[:, None] == target[None, :]
    ).astype(jnp.bfloat16)
    place_rows = jnp.sum(place_hot.reshape(experts * capacity, tok_count, 2), axis=-1)
    outgoing = jnp.dot(place_rows, normed, preferred_element_type=jnp.float32).astype(jnp.bfloat16)
    outgoing = outgoing.reshape(experts, capacity, width)
    chunks = 2
    chunk_slots = capacity // chunks
    arrivals = [
        lax.all_to_all(
            outgoing[:, c * chunk_slots : (c + 1) * chunk_slots],
            "expert",
            split_axis=0,
            concat_axis=0,
            tiled=True,
        ).reshape(-1, width)
        for c in range(chunks)
    ]
    first = lax.all_gather(arrivals[0], "leaf", axis=0, tiled=True)
    spread = leaf_spread(arrivals[1])
    first, share, *spread = lax.optimization_barrier((first, share, *spread))
    other_share = lax.ppermute(share, "tensor", perm=[(0, 1), (1, 0)])
    pieces_in = [first, jnp.concatenate(spread, axis=0)]
    returned = []
    for c in range(chunks):
        piece = pieces_in[c]
        if c == 1:
            piece, other_share = lax.optimization_barrier((piece, other_share))
        gate_v = jnp.dot(piece, w_gate[0], preferred_element_type=jnp.float32)
        up_v = jnp.dot(piece, w_up[0], preferred_element_type=jnp.float32)
        hidden = (jax.nn.silu(gate_v) * up_v).astype(jnp.bfloat16)
        down = jnp.dot(hidden, w_down[0], preferred_element_type=jnp.float32).astype(jnp.bfloat16)
        if c != 0:
            blocks = down.reshape(lax.axis_size("leaf"), -1, width)
            down = jnp.take(blocks, leaf_order(), axis=0).reshape(-1, width)
        part_rows = lax.psum_scatter(down, "leaf", scatter_dimension=0, tiled=True)
        returned.append(
            lax.all_to_all(
                part_rows.reshape(experts, chunk_slots, width),
                "expert",
                split_axis=0,
                concat_axis=0,
                tiled=True,
            )
        )
    back = jnp.concatenate(returned, axis=1).reshape(-1, width)
    low = lax.axis_index("tensor") == 0
    merged = jnp.concatenate(
        [jnp.where(low, share, other_share), jnp.where(low, other_share, share)], axis=0
    )
    picked = jnp.take(back, target, axis=0)
    picked = picked.astype(jnp.float32).reshape(tok_count, 2, width)
    own_mix = (gates[:, 0:1] * picked[:, 0] + gates[:, 1:2] * picked[:, 1]).astype(jnp.bfloat16)
    other_mix = lax.ppermute(own_mix, "tensor", perm=[(0, 1), (1, 0)])
    mixed = own_mix.astype(jnp.float32) + other_mix.astype(jnp.float32)
    return merged + mixed


def solution(mesh):
    in_specs = (
        P("leaf", ("expert", "tensor")),
        P("leaf", ("expert", "tensor")),
        P(),
        P("leaf"),
        P(("expert", "tensor"), None),
        P(("expert", "tensor"), None),
        P(),
        P(),
        P(("leaf", "expert"), None),
        P("expert", None, ("leaf", "tensor")),
        P("expert", None, ("leaf", "tensor")),
        P("expert", ("leaf", "tensor"), None),
    )
    out_specs = P(("leaf", "expert"), None)
    return jax.shard_map(
        per_device, mesh=mesh, in_specs=in_specs, out_specs=out_specs, check_vma=False
    )
```

```python
import math

import jax
import jax.numpy as jnp
from jax import lax
from jax.sharding import PartitionSpec as P

R = 256


def attend_parent(queries, keys, key_spans, span_bias, scale):
    rows, local_width = queries.shape
    heads_here, span_count = span_bias.shape
    head_size = local_width // heads_here
    key_count = keys.shape[0]
    q = queries.reshape(rows, heads_here, head_size)
    k = keys.reshape(key_count, heads_here, head_size)
    scores = jnp.einsum("qhd,khd->hqk", q, k, preferred_element_type=jnp.float32) * scale
    span_hot = (key_spans[:, None] == jnp.arange(span_count, dtype=jnp.int32)[None, :]).astype(
        jnp.float32
    )
    bias = jnp.dot(span_hot, span_bias.T, precision=lax.Precision.HIGHEST)
    scores = scores + bias.T[:, None, :]
    top = jnp.max(scores, axis=-1, keepdims=True)
    weights = jnp.exp(scores - top)
    total = jnp.sum(weights, axis=-1, keepdims=True)
    high = weights.astype(jnp.bfloat16)
    low = (weights - high.astype(jnp.float32)).astype(jnp.bfloat16)
    values = jnp.einsum("hqk,khd->hqd", high, k, preferred_element_type=jnp.float32) + jnp.einsum(
        "hqk,khd->hqd", low, k, preferred_element_type=jnp.float32
    )
    return (values / total).transpose(1, 0, 2).reshape(rows, local_width).astype(jnp.bfloat16)


def pair_gather(share):
    other = lax.ppermute(share, "tensor", perm=[(0, 1), (1, 0)])
    low = lax.axis_index("tensor") == 0
    return jnp.concatenate([jnp.where(low, share, other), jnp.where(low, other, share)], axis=0)


def per_device(
    drafts,
    children,
    child_order,
    spans,
    span_bias,
    out_weight,
    norm_gain,
    router,
    routes,
    w_gate,
    w_up,
    w_down,
):
    local_rows, local_width = drafts.shape
    heads_here = span_bias.shape[0]
    head_size = local_width // heads_here
    width = out_weight.shape[1]
    scale = 1.0 / math.sqrt(head_size)
    parents_here = local_rows // R
    leaf_index = lax.axis_index("leaf")
    child_rows = children.shape[0]
    children_here = child_rows // R
    span_rows = -(-spans.shape[0] // local_width)
    span_rows = -(-span_rows // 8) * 8
    span_block = jnp.pad(spans.astype(jnp.bfloat16), (0, span_rows * local_width - spans.shape[0]))
    payload = jnp.concatenate([children, span_block.reshape(span_rows, local_width)], axis=0)
    n_leaf = lax.axis_size("leaf")
    n_z = n_leaf // 2
    core = leaf_index % 2
    z = leaf_index // 2
    got = [payload]
    for k in range(1, n_z):
        perm = [(a * 2 + b, ((a + k) % n_z) * 2 + b) for a in range(n_z) for b in range(2)]
        got.append(lax.ppermute(payload, "leaf", perm=perm))
    swap = [(j, j ^ 1) for j in range(n_leaf)]
    got = got + [lax.ppermute(block, "leaf", perm=swap) for block in got]
    gathered = jnp.stack(got)
    span_table = gathered[:, child_rows:].reshape(gathered.shape[0], span_rows * local_width)
    count = child_order.shape[0]
    ids = jnp.arange(count, dtype=jnp.int32)
    inverse = jnp.sum(jnp.where(child_order[None, :] == ids[:, None], ids[None, :], 0), axis=1)

    def child_keys(child):
        owner = child // children_here
        slot = jnp.where(owner % 2 == core, 0, n_z) + (z - owner // 2) % n_z
        offset = (child % children_here) * R
        rows = lax.dynamic_slice(gathered, (slot, offset, 0), (1, R, local_width))[0]
        marks = lax.dynamic_slice(span_table, (slot, offset), (1, R))[0]
        return rows, marks.astype(jnp.int32)

    pieces = []
    for i in range(parents_here):
        parent = leaf_index * parents_here + i
        first_rows, first_spans = child_keys(inverse[2 * parent])
        second_rows, second_spans = child_keys(inverse[2 * parent + 1])
        own_keys = jnp.concatenate([first_rows, second_rows], axis=0)
        own_spans = jnp.concatenate([first_spans, second_spans], axis=0)
        pieces.append(attend_parent(drafts[i * R : (i + 1) * R], own_keys, own_spans, span_bias, scale))
    attended = pieces[0] if parents_here == 1 else jnp.concatenate(pieces, axis=0)
    term = jnp.dot(attended, out_weight, preferred_element_type=jnp.float32)
    offset = lax.axis_index(("expert", "tensor")) * local_width
    own_cols = lax.dynamic_slice(term, (0, offset), (local_rows, local_width)) + drafts.astype(
        jnp.float32
    )
    term = lax.dynamic_update_slice(term, own_cols, (0, offset)).astype(jnp.bfloat16)
    group = lax.axis_size(("expert", "tensor"))
    share_rows = local_rows // group
    arrived_terms = lax.all_to_all(
        term.reshape(group, share_rows, width), ("expert", "tensor"), 0, 0, tiled=True
    )
    share = jnp.sum(arrived_terms.astype(jnp.float32), axis=0)
    mean_square = jnp.mean(share * share, axis=-1, keepdims=True)
    normed = pair_gather((share * lax.rsqrt(mean_square + 1e-05) * norm_gain).astype(jnp.bfloat16))
    logits = jnp.dot(normed, router, preferred_element_type=jnp.float32)
    experts = router.shape[1]
    tok_count = routes.shape[0]
    capacity = 4 * tok_count // lax.axis_size("expert")
    choice_hot = routes[:, :, None] == jnp.arange(experts, dtype=jnp.int32)[None, None, :]
    chosen = jnp.sum(jnp.where(choice_hot, logits[:, None, :], 0.0), axis=-1)
    gates = jax.nn.softmax(chosen, axis=-1)
    pairs = routes.reshape(-1)
    pair_hot = (pairs[:, None] == jnp.arange(experts, dtype=jnp.int32)[None, :]).astype(jnp.int32)
    earlier = jnp.cumsum(pair_hot, axis=0) - pair_hot
    slot_index = jnp.sum(earlier * pair_hot, axis=1)
    target = pairs * capacity + slot_index
    place_hot = (
        jnp.arange(experts * capacity, dtype=jnp.int32)[:, None] == target[None, :]
    ).astype(jnp.bfloat16)
    place_rows = jnp.sum(place_hot.reshape(experts * capacity, tok_count, 2), axis=-1)
    outgoing = jnp.dot(place_rows, normed, preferred_element_type=jnp.float32).astype(jnp.bfloat16)
    outgoing = outgoing.reshape(experts, capacity, width)
    chunks = 2
    chunk_slots = capacity // chunks
    returned = []
    for c in range(chunks):
        arrived = lax.all_to_all(
            outgoing[:, c * chunk_slots : (c + 1) * chunk_slots],
            "expert",
            split_axis=0,
            concat_axis=0,
            tiled=True,
        ).reshape(-1, width)
        piece = lax.all_gather(arrived, "leaf", axis=0, tiled=True)
        if c == 0:
            piece, share = lax.optimization_barrier((piece, share))
            other_share = lax.ppermute(share, "tensor", perm=[(0, 1), (1, 0)])
        else:
            piece, other_share = lax.optimization_barrier((piece, other_share))
        gate_v = jnp.dot(piece, w_gate[0], preferred_element_type=jnp.float32)
        up_v = jnp.dot(piece, w_up[0], preferred_element_type=jnp.float32)
        hidden = (jax.nn.silu(gate_v) * up_v).astype(jnp.bfloat16)
        down = jnp.dot(hidden, w_down[0], preferred_element_type=jnp.float32).astype(jnp.bfloat16)
        part_rows = lax.psum_scatter(down, "leaf", scatter_dimension=0, tiled=True)
        returned.append(
            lax.all_to_all(
                part_rows.reshape(experts, chunk_slots, width),
                "expert",
                split_axis=0,
                concat_axis=0,
                tiled=True,
            )
        )
    back = jnp.concatenate(returned, axis=1).reshape(-1, width)
    low = lax.axis_index("tensor") == 0
    merged = jnp.concatenate(
        [jnp.where(low, share, other_share), jnp.where(low, other_share, share)], axis=0
    )
    picked = jnp.take(back, target, axis=0)
    picked = picked.astype(jnp.float32).reshape(tok_count, 2, width)
    own_mix = (gates[:, 0:1] * picked[:, 0] + gates[:, 1:2] * picked[:, 1]).astype(jnp.bfloat16)
    other_mix = lax.ppermute(own_mix, "tensor", perm=[(0, 1), (1, 0)])
    mixed = own_mix.astype(jnp.float32) + other_mix.astype(jnp.float32)
    return merged + mixed


def solution(mesh):
    in_specs = (
        P("leaf", ("expert", "tensor")),
        P("leaf", ("expert", "tensor")),
        P(),
        P("leaf"),
        P(("expert", "tensor"), None),
        P(("expert", "tensor"), None),
        P(),
        P(),
        P(("leaf", "expert"), None),
        P("expert", None, ("leaf", "tensor")),
        P("expert", None, ("leaf", "tensor")),
        P("expert", ("leaf", "tensor"), None),
    )
    out_specs = P(("leaf", "expert"), None)
    return jax.shard_map(
        per_device, mesh=mesh, in_specs=in_specs, out_specs=out_specs, check_vma=False
    )
```

```python
import math

import jax
import jax.numpy as jnp
from jax import lax
from jax.sharding import PartitionSpec as P

R = 256


def attend_parent(queries, keys, key_spans, span_bias, scale):
    rows, local_width = queries.shape
    heads_here, span_count = span_bias.shape
    head_size = local_width // heads_here
    key_count = keys.shape[0]
    q = queries.reshape(rows, heads_here, head_size)
    k = keys.reshape(key_count, heads_here, head_size)
    scores = jnp.einsum("qhd,khd->hqk", q, k, preferred_element_type=jnp.float32) * scale
    bias = jnp.take(span_bias, key_spans, axis=1)
    scores = scores + bias[:, None, :]
    top = jnp.max(scores, axis=-1, keepdims=True)
    weights = jnp.exp(scores - top)
    total = jnp.sum(weights, axis=-1, keepdims=True)
    high = weights.astype(jnp.bfloat16)
    low = (weights - high.astype(jnp.float32)).astype(jnp.bfloat16)
    values = jnp.einsum("hqk,khd->hqd", high, k, preferred_element_type=jnp.float32) + jnp.einsum(
        "hqk,khd->hqd", low, k, preferred_element_type=jnp.float32
    )
    return (values / total).transpose(1, 0, 2).reshape(rows, local_width).astype(jnp.bfloat16)


def pair_gather(share):
    other = lax.ppermute(share, "tensor", perm=[(0, 1), (1, 0)])
    low = lax.axis_index("tensor") == 0
    return jnp.concatenate([jnp.where(low, share, other), jnp.where(low, other, share)], axis=0)


def per_device(
    drafts,
    children,
    child_order,
    spans,
    span_bias,
    out_weight,
    norm_gain,
    router,
    routes,
    w_gate,
    w_up,
    w_down,
):
    local_rows, local_width = drafts.shape
    heads_here = span_bias.shape[0]
    head_size = local_width // heads_here
    width = out_weight.shape[1]
    scale = 1.0 / math.sqrt(head_size)
    parents_here = local_rows // R
    leaf_index = lax.axis_index("leaf")
    child_rows = children.shape[0]
    children_here = child_rows // R
    span_rows = -(-spans.shape[0] // local_width)
    span_rows = -(-span_rows // 8) * 8
    span_block = jnp.pad(spans.astype(jnp.bfloat16), (0, span_rows * local_width - spans.shape[0]))
    payload = jnp.concatenate([children, span_block.reshape(span_rows, local_width)], axis=0)
    n_leaf = lax.axis_size("leaf")
    n_z = n_leaf // 2
    core = leaf_index % 2
    z = leaf_index // 2
    got = [payload]
    for k in range(1, n_z):
        perm = [(a * 2 + b, ((a + k) % n_z) * 2 + b) for a in range(n_z) for b in range(2)]
        got.append(lax.ppermute(payload, "leaf", perm=perm))
    swap = [(j, j ^ 1) for j in range(n_leaf)]
    got = got + [lax.ppermute(block, "leaf", perm=swap) for block in got]
    gathered = jnp.stack(got)
    span_table = gathered[:, child_rows:].reshape(gathered.shape[0], span_rows * local_width)
    count = child_order.shape[0]
    ids = jnp.arange(count, dtype=jnp.int32)
    inverse = jnp.sum(jnp.where(child_order[None, :] == ids[:, None], ids[None, :], 0), axis=1)

    def child_keys(child):
        owner = child // children_here
        slot = jnp.where(owner % 2 == core, 0, n_z) + (z - owner // 2) % n_z
        offset = (child % children_here) * R
        rows = lax.dynamic_slice(gathered, (slot, offset, 0), (1, R, local_width))[0]
        marks = lax.dynamic_slice(span_table, (slot, offset), (1, R))[0]
        return rows, marks.astype(jnp.int32)

    pieces = []
    for i in range(parents_here):
        parent = leaf_index * parents_here + i
        first_rows, first_spans = child_keys(inverse[2 * parent])
        second_rows, second_spans = child_keys(inverse[2 * parent + 1])
        own_keys = jnp.concatenate([first_rows, second_rows], axis=0)
        own_spans = jnp.concatenate([first_spans, second_spans], axis=0)
        pieces.append(attend_parent(drafts[i * R : (i + 1) * R], own_keys, own_spans, span_bias, scale))
    attended = pieces[0] if parents_here == 1 else jnp.concatenate(pieces, axis=0)
    term = jnp.dot(attended, out_weight, preferred_element_type=jnp.float32)
    offset = lax.axis_index(("expert", "tensor")) * local_width
    own_cols = lax.dynamic_slice(term, (0, offset), (local_rows, local_width)) + drafts.astype(
        jnp.float32
    )
    term = lax.dynamic_update_slice(term, own_cols, (0, offset)).astype(jnp.bfloat16)
    group = lax.axis_size(("expert", "tensor"))
    share_rows = local_rows // group
    arrived_terms = lax.all_to_all(
        term.reshape(group, share_rows, width), ("expert", "tensor"), 0, 0, tiled=True
    )
    share = jnp.sum(arrived_terms.astype(jnp.float32), axis=0)
    mean_square = jnp.mean(share * share, axis=-1, keepdims=True)
    normed = pair_gather((share * lax.rsqrt(mean_square + 1e-05) * norm_gain).astype(jnp.bfloat16))
    logits = jnp.dot(normed, router, preferred_element_type=jnp.float32)
    experts = router.shape[1]
    tok_count = routes.shape[0]
    capacity = 4 * tok_count // lax.axis_size("expert")
    choice_hot = routes[:, :, None] == jnp.arange(experts, dtype=jnp.int32)[None, None, :]
    chosen = jnp.sum(jnp.where(choice_hot, logits[:, None, :], 0.0), axis=-1)
    gates = jax.nn.softmax(chosen, axis=-1)
    pairs = routes.reshape(-1)
    pair_hot = (pairs[:, None] == jnp.arange(experts, dtype=jnp.int32)[None, :]).astype(jnp.int32)
    earlier = jnp.cumsum(pair_hot, axis=0) - pair_hot
    slot_index = jnp.sum(earlier * pair_hot, axis=1)
    target = pairs * capacity + slot_index
    place_hot = (
        jnp.arange(experts * capacity, dtype=jnp.int32)[:, None] == target[None, :]
    ).astype(jnp.bfloat16)
    place_rows = jnp.sum(place_hot.reshape(experts * capacity, tok_count, 2), axis=-1)
    outgoing = jnp.dot(place_rows, normed, preferred_element_type=jnp.float32).astype(jnp.bfloat16)
    outgoing = outgoing.reshape(experts, capacity, width)
    chunks = 2
    chunk_slots = capacity // chunks
    returned = []
    for c in range(chunks):
        arrived = lax.all_to_all(
            outgoing[:, c * chunk_slots : (c + 1) * chunk_slots],
            "expert",
            split_axis=0,
            concat_axis=0,
            tiled=True,
        ).reshape(-1, width)
        piece = lax.all_gather(arrived, "leaf", axis=0, tiled=True)
        if c == 0:
            piece, share = lax.optimization_barrier((piece, share))
            other_share = lax.ppermute(share, "tensor", perm=[(0, 1), (1, 0)])
        else:
            piece, other_share = lax.optimization_barrier((piece, other_share))
        gate_v = jnp.dot(piece, w_gate[0], preferred_element_type=jnp.float32)
        up_v = jnp.dot(piece, w_up[0], preferred_element_type=jnp.float32)
        hidden = (jax.nn.silu(gate_v) * up_v).astype(jnp.bfloat16)
        down = jnp.dot(hidden, w_down[0], preferred_element_type=jnp.float32).astype(jnp.bfloat16)
        part_rows = lax.psum_scatter(down, "leaf", scatter_dimension=0, tiled=True)
        returned.append(
            lax.all_to_all(
                part_rows.reshape(experts, chunk_slots, width),
                "expert",
                split_axis=0,
                concat_axis=0,
                tiled=True,
            )
        )
    back = jnp.concatenate(returned, axis=1).reshape(-1, width)
    low = lax.axis_index("tensor") == 0
    merged = jnp.concatenate(
        [jnp.where(low, share, other_share), jnp.where(low, other_share, share)], axis=0
    )
    picked = jnp.take(back, target, axis=0)
    picked = picked.astype(jnp.float32).reshape(tok_count, 2, width)
    own_mix = (gates[:, 0:1] * picked[:, 0] + gates[:, 1:2] * picked[:, 1]).astype(jnp.bfloat16)
    other_mix = lax.ppermute(own_mix, "tensor", perm=[(0, 1), (1, 0)])
    mixed = own_mix.astype(jnp.float32) + other_mix.astype(jnp.float32)
    return merged + mixed


def solution(mesh):
    in_specs = (
        P("leaf", ("expert", "tensor")),
        P("leaf", ("expert", "tensor")),
        P(),
        P("leaf"),
        P(("expert", "tensor"), None),
        P(("expert", "tensor"), None),
        P(),
        P(),
        P(("leaf", "expert"), None),
        P("expert", None, ("leaf", "tensor")),
        P("expert", None, ("leaf", "tensor")),
        P("expert", ("leaf", "tensor"), None),
    )
    out_specs = P(("leaf", "expert"), None)
    return jax.shard_map(
        per_device, mesh=mesh, in_specs=in_specs, out_specs=out_specs, check_vma=False
    )
```
